128 devices in a mesh: req: 4 (over y), head: 8 (over z, x_hi), blk: 4 (over x_lo, core).
Axes of the slice: x: 4 (x_hi: 2, x_lo: 2; x = x_hi * 2 + x_lo), y: 4, z: 4, core: 2. Of those that a mesh axis runs over, the one named last changes fastest.
Arguments:
- image_hidden: bfloat16 [16, 32, 32, 1536], P('req', 'head', 'blk'), parts along dimension 0, may hold values from -6 to 6
- text_hidden: bfloat16 [16, 160, 1536], P('req', ('head', 'blk')), parts along dimension 0, may hold values from -6 to 6
- latent_grid: float32 [16, 64, 64, 16], P('req', 'head', 'blk'), parts along dimension 0, may hold values from -6 to 6
- text_lengths: int32 [16], P('req'), parts along dimension 0, may hold values from 38 to 154, as said below
- step_index: int32 [16], P('req'), parts along dimension 0, may hold values from 125 to 999
- image_mod: float32 [16, 6, 1536], P('req'), parts along dimension 0, may hold values from -3 to 3
- text_mod: float32 [16, 6, 1536], P('req'), parts along dimension 0, may hold values from -3 to 3
- final_mod: float32 [16, 2, 1536], P('req'), parts along dimension 0, may hold values from -3 to 3
- image_qk_gain: float32 [2, 64], replicated, may hold values from 0.5 to 2.3
- text_qk_gain: float32 [2, 64], replicated, may hold values from 0.5 to 2.3
- image_qkv: bfloat16 [1536, 3, 1536], P(None, None, 'head'), may hold values from -0.15625 to 0.15625
- text_qkv: bfloat16 [1536, 3, 1536], P(None, None, 'head'), may hold values from -0.15625 to 0.15625
- image_proj: bfloat16 [1536, 1536], P('head'), may hold values from -0.15625 to 0.15625
- text_proj: bfloat16 [1536, 1536], P('head'), may hold values from -0.15625 to 0.15625
- image_up: bfloat16 [1536, 6144], P(None, 'head'), may hold values from -0.15625 to 0.15625
- text_up: bfloat16 [1536, 6144], P(None, 'head'), may hold values from -0.15625 to 0.15625
- image_down: bfloat16 [6144, 1536], P('head'), may hold values from -0.078125 to 0.078125
- text_down: bfloat16 [6144, 1536], P('head'), may hold values from -0.078125 to 0.078125
- final_proj: bfloat16 [1536, 64], replicated, may hold values from -0.15625 to 0.15625
- conv_kernel: bfloat16 [3, 3, 16, 512], replicated, may hold values from -0.5 to 0.5
Outputs:
- image_states: bfloat16 [16, 32, 32, 1536], P('req', 'head', 'blk'), parts along dimension 0
- text_states: bfloat16 [16, 160, 1536], P('req', ('head', 'blk')), parts along dimension 0
- latent_next: float32 [16, 64, 64, 16], P('req', 'head', 'blk'), parts along dimension 0
- features: bfloat16 [16, 64, 64, 512], P('req', 'head', 'blk'), parts along dimension 0
The draws below stay inside these ranges and needn't reach their ends.
There are 4 independent parts, one for each index of `req`. The reference program is written for one: setup_inputs(seed, part) draws one part's arguments, and reference() takes and returns one part's arrays. A program takes and returns all parts, laid end to end along the dimension named above; an argument that names none is the same for every part. Nothing has to cross between parts.
Inputs may be any that keep to these rules, and one draw needn't show every extreme that they name: `text_lengths`: every request has 154 or fewer live text tokens, and in each group one request has exactly 154.
All inputs are finite; a program needn't handle non-finite values.
Results may differ from the reference program's by a relative error of at most 0.012.
Values may be sent and summed in bfloat16 or wider, within the bound.
No kernel may reach another device: no remote copies, remote signals or barrier semaphores. Data moves between devices by JAX's collectives and lax.ppermute only.
A program may use at most 128 MiB of HBM per device.

```python
import jax
import jax.numpy as jnp
from jax import lax

D = 1536
HEADS = 24
HD = 64
FF = 6144
LC = 16
CONV = 512
PC = 64
GRID = 32
TXT = 160
TXT_MAX = 154
REQ = 4


def draw_text_lengths(key, part):
    first_key, second_key = jax.random.split(jax.random.fold_in(key, 17))
    drawn = jax.random.randint(first_key, (REQ,), TXT_MAX // 4, TXT_MAX + 1)
    chosen = jax.random.randint(second_key, (), 0, REQ)
    return jnp.where(jnp.arange(REQ) == chosen, TXT_MAX, drawn).astype(jnp.int32)


def touch_ends(values, rng, smallest, top_value):
    longest = values.shape.index(max(values.shape))
    spots = []
    for shift in (0, 1):
        where = [jax.random.randint(jax.random.fold_in(rng, axis), (), 0, length) for axis, length in enumerate(values.shape)]
        where[longest] = (where[longest] + shift) % values.shape[longest]
        spots.append(tuple(where))
    return values.at[spots[0]].set(smallest).at[spots[1]].set(top_value)


def block_levels(own_key, extent, shards, smallest, largest):
    def one(dim, blocks):
        steps = jax.random.uniform(jax.random.fold_in(jax.random.fold_in(own_key, 6), dim), (blocks,), jnp.float32, smallest / len(shards), largest / len(shards))
        return jnp.repeat(jnp.exp(steps), extent[dim] // blocks).reshape((-1,) + (1,) * (len(extent) - dim - 1))

    level = one(*shards[0])
    for cut in shards[1:]:
        level = level * one(*cut)
    return level


def bell_draw(own_key, dims, scale, most, cuts=(), held_as=jnp.bfloat16):
    values = scale * jax.random.normal(own_key, dims, jnp.float32)
    if cuts:
        values = values * block_levels(own_key, dims, cuts, -0.22, 0.18)
    return jnp.clip(values, -most, most).astype(held_as)


def setup_inputs(seed: int = 0, part: int = 0) -> dict:
    splits = jax.random.split(jax.random.key(seed), 21)
    part_splits = jax.random.split(jax.random.fold_in(splits[20], part), 21)
    return {
        "image_hidden": bell_draw(part_splits[0], (REQ, GRID, GRID, D), 1.0, 6.0, ((1, 8), (2, 4))),
        "text_hidden": bell_draw(part_splits[1], (REQ, TXT, D), 1.0, 6.0, ((1, 32),)),
        "latent_grid": bell_draw(part_splits[2], (REQ, 2 * GRID, 2 * GRID, LC), 1.0, 6.0, ((1, 8), (2, 4)), jnp.float32),
        "text_lengths": draw_text_lengths(jax.random.fold_in(jax.random.fold_in(splits[20], part), 71), part),
        "step_index": touch_ends(jax.random.randint(part_splits[4], (REQ,), 125, 1000), jax.random.fold_in(part_splits[4], 1), 125, 999).astype(jnp.int32),
        "image_mod": bell_draw(part_splits[5], (REQ, 6, D), 0.5, 3.0, (), jnp.float32),
        "text_mod": bell_draw(part_splits[6], (REQ, 6, D), 0.5, 3.0, (), jnp.float32),
        "final_mod": bell_draw(part_splits[7], (REQ, 2, D), 0.5, 3.0, (), jnp.float32),
        "image_qk_gain": jnp.clip(jax.random.uniform(splits[8], (2, HD), jnp.float32, 0.5, 2.3), 0.5, 2.3),
        "text_qk_gain": jnp.clip(jax.random.uniform(splits[9], (2, HD), jnp.float32, 0.5, 2.3), 0.5, 2.3),
        "image_qkv": bell_draw(splits[10], (D, 3, HEADS * HD), D ** -0.5, 0.15625, ((2, 8),)),
        "text_qkv": bell_draw(splits[11], (D, 3, HEADS * HD), D ** -0.5, 0.15625, ((2, 8),)),
        "image_proj": bell_draw(splits[12], (HEADS * HD, D), D ** -0.5, 0.15625, ((0, 8),)),
        "text_proj": bell_draw(splits[13], (HEADS * HD, D), D ** -0.5, 0.15625, ((0, 8),)),
        "image_up": bell_draw(splits[14], (D, FF), D ** -0.5, 0.15625, ((1, 8),)),
        "text_up": bell_draw(splits[15], (D, FF), D ** -0.5, 0.15625, ((1, 8),)),
        "image_down": bell_draw(splits[16], (FF, D), FF ** -0.5, 0.078125, ((0, 8),)),
        "text_down": bell_draw(splits[17], (FF, D), FF ** -0.5, 0.078125, ((0, 8),)),
        "final_proj": bell_draw(splits[18], (D, PC), D ** -0.5, 0.15625),
        "conv_kernel": bell_draw(splits[19], (3, 3, LC, CONV), (9 * LC) ** -0.5, 0.5),
    }


def widen(values):
    return lax.optimization_barrier(values.astype(jnp.bfloat16)).astype(jnp.float32)

def expand(vector, values):
    return vector.reshape((vector.shape[0],) + (1,) * (values.ndim - 2) + (vector.shape[-1],))

def modulate(values, shift, scale):
    average = lax.optimization_barrier(jnp.mean(values, -1, keepdims=True))
    centred = values - average
    spread = lax.optimization_barrier(jnp.mean(centred * centred, -1, keepdims=True))
    normed = centred * lax.rsqrt(spread + 1e-06)
    return normed * (1.0 + expand(scale, values)) + expand(shift, values)

def head_norm(values, gain):
    shaped = values.reshape(values.shape[:-1] + (HEADS, HD))
    return widen(shaped * lax.rsqrt(lax.optimization_barrier(jnp.mean(shaped * shaped, -1, keepdims=True)) + 1e-06) * gain)

def noise_level(fraction):
    return 3.0 * fraction / (1.0 + 2.0 * fraction)

def attention_inputs(normed, weight, gains):
    projected = jnp.einsum('rnd,dje->rnje', normed, weight.astype(jnp.float32))
    queries = head_norm(projected[:, :, 0], gains[0])
    key_heads = head_norm(projected[:, :, 1], gains[1])
    value_heads = widen(projected[:, :, 2].reshape(queries.shape))
    return (queries, key_heads, value_heads)

def reference(image_hidden, text_hidden, latent_grid, text_lengths, step_index, image_mod, text_mod, final_mod, image_qk_gain, text_qk_gain, image_qkv, text_qkv, image_proj, text_proj, image_up, text_up, image_down, text_down, final_proj, conv_kernel):
    image_rows = GRID * GRID
    image_flat = image_hidden.astype(jnp.float32).reshape(REQ, image_rows, D)
    text_flat = text_hidden.astype(jnp.float32)
    image_norm = widen(modulate(image_flat, image_mod[:, 0], image_mod[:, 1]))
    text_norm = widen(modulate(text_flat, text_mod[:, 0], text_mod[:, 1]))
    image_q, image_k, image_v = attention_inputs(image_norm, image_qkv, image_qk_gain)
    text_q, text_k, text_v = attention_inputs(text_norm, text_qkv, text_qk_gain)
    queries = jnp.concatenate([image_q, text_q], 1)
    key_heads = jnp.concatenate([image_k, text_k], 1)
    value_heads = jnp.concatenate([image_v, text_v], 1)
    slot_ids = jnp.arange(TXT, dtype=jnp.int32)
    score_scale = 1.0 / HD ** 0.5

    def attend_one(items):
        query_one, key_one, value_one, length = items
        usable = jnp.concatenate([jnp.ones((image_rows,), jnp.float32), (slot_ids < length).astype(jnp.float32)])
        scores = jnp.einsum('qhd,khd->hqk', query_one, key_one) * score_scale
        weights = jnp.exp(scores) * usable[None, None, :]
        denominator = lax.optimization_barrier(jnp.sum(weights, -1))
        numerator = jnp.einsum('hqk,khd->hqd', widen(weights), value_one)
        context = (numerator / denominator[:, :, None]).astype(jnp.bfloat16)
        return context.transpose(1, 0, 2).reshape(image_rows + TXT, HEADS * HD)
    context = lax.map(attend_one, (queries, key_heads, value_heads, text_lengths))
    context = widen(context)
    image_attn = jnp.einsum('rne,ed->rnd', context[:, :image_rows], image_proj.astype(jnp.float32))
    text_attn = jnp.einsum('rne,ed->rnd', context[:, image_rows:], text_proj.astype(jnp.float32))
    image_mid = image_flat + expand(image_mod[:, 2], image_attn) * image_attn
    text_mid = text_flat + expand(text_mod[:, 2], text_attn) * text_attn
    image_in = widen(modulate(image_mid, image_mod[:, 3], image_mod[:, 4]))
    text_in = widen(modulate(text_mid, text_mod[:, 3], text_mod[:, 4]))
    image_hid = widen(jax.nn.gelu(jnp.einsum('rnd,df->rnf', image_in, image_up.astype(jnp.float32)), approximate=True))
    text_hid = widen(jax.nn.gelu(jnp.einsum('rnd,df->rnf', text_in, text_up.astype(jnp.float32)), approximate=True))
    image_back = jnp.einsum('rnf,fd->rnd', image_hid, image_down.astype(jnp.float32))
    text_back = jnp.einsum('rnf,fd->rnd', text_hid, text_down.astype(jnp.float32))
    image_out = image_mid + expand(image_mod[:, 5], image_back) * image_back
    image_states = image_out.reshape(REQ, GRID, GRID, D).astype(jnp.bfloat16)
    text_states = (text_mid + expand(text_mod[:, 5], text_back) * text_back).astype(jnp.bfloat16)
    final_in = widen(modulate(image_out, final_mod[:, 1], final_mod[:, 0]))
    velocity = jnp.einsum('rnd,dp->rnp', final_in, final_proj.astype(jnp.float32))
    velocity = velocity.reshape(REQ, GRID, GRID, 2, 2, LC).transpose(0, 1, 3, 2, 4, 5).reshape(REQ, 2 * GRID, 2 * GRID, LC)
    current = step_index.astype(jnp.float32) / 1000.0
    following = jnp.maximum(step_index - 125, 0).astype(jnp.float32) / 1000.0
    step_size = noise_level(following) - noise_level(current)
    latent_next = latent_grid + step_size[:, None, None, None] * velocity
    decoded_in = widen(latent_next / 1.5305 + 0.0609)
    padded = jnp.pad(decoded_in, ((0, 0), (1, 1), (1, 1), (0, 0)))
    out_rows = 2 * GRID
    summed = jnp.zeros((REQ, out_rows, out_rows, CONV), jnp.float32)
    kernel_wide = conv_kernel.astype(jnp.float32)
    for row_off in range(3):
        for col_off in range(3):
            summed = summed + jnp.einsum('rhwc,co->rhwo', padded[:, row_off:row_off + out_rows, col_off:col_off + out_rows], kernel_wide[row_off, col_off])
    return (image_states, text_states, latent_next, summed.astype(jnp.bfloat16))
```

```python
import math

import jax
import jax.numpy as jnp
from jax import lax
from jax.sharding import PartitionSpec as P

HD = 64


def extended(block, sides, width):
    for axis, dim in sides:
        count = lax.axis_size(axis)
        forward = [(i, i + 1) for i in range(count - 1)]
        backward = [(target, source) for source, target in forward]
        low = lax.ppermute(
            lax.slice_in_dim(block, block.shape[dim] - width, None, axis=dim), axis, forward
        )
        high = lax.ppermute(lax.slice_in_dim(block, 0, width, axis=dim), axis, backward)
        block = jnp.concatenate([low, block, high], axis=dim)
    return block


def per_request(vector, values, axis):
    shape = [1] * values.ndim
    shape[axis] = vector.shape[0]
    shape[-1] = vector.shape[-1]
    return vector.reshape(shape)


def modulate(values, shift, scale, axis):
    average = jnp.mean(values, -1, keepdims=True)
    centred = values - average
    spread = jnp.mean(centred * centred, -1, keepdims=True)
    normed = centred * lax.rsqrt(spread + 1e-06)
    return normed * (1.0 + per_request(scale, values, axis)) + per_request(shift, values, axis)


def head_norm(values, gain):
    shaped = values.reshape(values.shape[:-1] + (values.shape[-1] // HD, HD))
    return (shaped * lax.rsqrt(jnp.mean(shaped * shaped, -1, keepdims=True) + 1e-06) * gain).astype(
        jnp.bfloat16
    )


def noise_level(fraction):
    return 3.0 * fraction / (1.0 + 2.0 * fraction)


def attention_inputs(normed, weight, gains):
    projected = jnp.einsum("arnd,dje->arnje", normed, weight, preferred_element_type=jnp.float32)
    queries = head_norm(projected[..., 0, :], gains[0])
    key_heads = head_norm(projected[..., 1, :], gains[1])
    value_heads = projected[..., 2, :].reshape(queries.shape).astype(jnp.bfloat16)
    return (queries, key_heads, value_heads)


def convolve(padded, kernel):
    out_rows = padded.shape[1] - 2
    out_cols = padded.shape[2] - 2
    summed = jnp.zeros((padded.shape[0], out_rows, out_cols, kernel.shape[-1]), jnp.float32)
    for row_off in range(3):
        for col_off in range(3):
            summed = summed + jnp.einsum(
                "rhwc,co->rhwo",
                padded[:, row_off : row_off + out_rows, col_off : col_off + out_cols],
                kernel[row_off, col_off],
                preferred_element_type=jnp.float32,
            )
    return summed.astype(jnp.bfloat16)


def body(
    image_hidden,
    text_hidden,
    latent_grid,
    text_lengths,
    step_index,
    image_mod,
    text_mod,
    final_mod,
    image_qk_gain,
    text_qk_gain,
    image_qkv,
    text_qkv,
    image_proj,
    text_proj,
    image_up,
    text_up,
    image_down,
    text_down,
    final_proj,
    conv_kernel,
):
    blocks = lax.axis_size("blk")
    groups = lax.axis_size("head")
    requests, tile_rows, tile_cols, model_width = image_hidden.shape
    text_slice = text_hidden.shape[1]
    image_tile = tile_rows * tile_cols
    tile_tokens = image_tile + text_slice
    own = jnp.concatenate(
        [image_hidden.reshape(requests, image_tile, model_width), text_hidden], axis=1
    )
    strip = lax.all_gather(own, "head", axis=0)
    strip_f = strip.astype(jnp.float32)
    image_x = strip_f[:, :, :image_tile]
    text_x = strip_f[:, :, image_tile:]
    image_norm = modulate(image_x, image_mod[:, 0], image_mod[:, 1], 1).astype(jnp.bfloat16)
    text_norm = modulate(text_x, text_mod[:, 0], text_mod[:, 1], 1).astype(jnp.bfloat16)
    image_q, image_k, image_v = attention_inputs(image_norm, image_qkv, image_qk_gain)
    text_q, text_k, text_v = attention_inputs(text_norm, text_qkv, text_qk_gain)
    queries = jnp.concatenate([image_q, text_q], 2)
    key_heads = jnp.concatenate([image_k, text_k], 2)
    value_heads = jnp.concatenate([image_v, text_v], 2)
    local_heads = queries.shape[3]
    score_scale = 1.0 / math.sqrt(HD)
    kv = lax.all_gather(jnp.stack([key_heads, value_heads]), "blk", axis=0)
    span = blocks * groups * tile_tokens
    key_piece = kv[:, 0].transpose(2, 4, 0, 1, 3, 5).reshape(requests, local_heads, span, HD)
    value_piece = kv[:, 1].transpose(2, 4, 0, 1, 3, 5).reshape(requests, local_heads, span, HD)
    query_rows = groups * tile_tokens
    query_piece = queries.transpose(1, 3, 0, 2, 4).reshape(requests, local_heads, query_rows, HD)
    position = jnp.arange(span, dtype=jnp.int32)
    source = position // (groups * tile_tokens)
    group = (position // tile_tokens) % groups
    within = position % tile_tokens
    slot_ids = (group * blocks + source) * text_slice + (within - image_tile)
    usable = (within < image_tile)[None, :] | (slot_ids[None, :] < text_lengths[:, None])
    scores = (
        jnp.einsum("rhqd,rhkd->rhqk", query_piece, key_piece, preferred_element_type=jnp.float32)
        * score_scale
    )
    weights = jnp.exp(scores) * usable[:, None, None, :].astype(jnp.float32)
    denominator = jnp.sum(weights, -1)
    numerator = jnp.einsum(
        "rhqk,rhkd->rhqd",
        weights.astype(jnp.bfloat16),
        value_piece,
        preferred_element_type=jnp.float32,
    )
    context = (numerator / denominator[..., None]).astype(jnp.bfloat16)
    local_width = local_heads * HD
    context = (
        context.reshape(requests, local_heads, groups, tile_tokens, HD)
        .transpose(2, 0, 3, 1, 4)
        .reshape(groups, requests, tile_tokens, local_width)
    )
    image_part = jnp.einsum(
        "arne,ed->arnd", context[:, :, :image_tile], image_proj, preferred_element_type=jnp.float32
    )
    text_part = jnp.einsum(
        "arne,ed->arnd", context[:, :, image_tile:], text_proj, preferred_element_type=jnp.float32
    )
    attn = lax.psum_scatter(
        jnp.concatenate([image_part, text_part], 2).astype(jnp.bfloat16),
        "head",
        scatter_dimension=0,
    ).astype(jnp.float32)
    own_f = own.astype(jnp.float32)
    image_mid = own_f[:, :image_tile] + per_request(image_mod[:, 2], own_f, 0) * attn[:, :image_tile]
    text_mid = own_f[:, image_tile:] + per_request(text_mod[:, 2], own_f, 0) * attn[:, image_tile:]
    image_local = modulate(image_mid, image_mod[:, 3], image_mod[:, 4], 0).astype(jnp.bfloat16)
    text_local = modulate(text_mid, text_mod[:, 3], text_mod[:, 4], 0).astype(jnp.bfloat16)
    ff_in = lax.all_gather(jnp.concatenate([image_local, text_local], 1), "head", axis=0)
    image_hid = jax.nn.gelu(
        jnp.einsum("arnd,df->arnf", ff_in[:, :, :image_tile], image_up, preferred_element_type=jnp.float32),
        approximate=True,
    ).astype(jnp.bfloat16)
    text_hid = jax.nn.gelu(
        jnp.einsum("arnd,df->arnf", ff_in[:, :, image_tile:], text_up, preferred_element_type=jnp.float32),
        approximate=True,
    ).astype(jnp.bfloat16)
    image_back = jnp.einsum("arnf,fd->arnd", image_hid, image_down, preferred_element_type=jnp.float32)
    text_back = jnp.einsum("arnf,fd->arnd", text_hid, text_down, preferred_element_type=jnp.float32)
    mlp = lax.psum_scatter(
        jnp.concatenate([image_back, text_back], 2).astype(jnp.bfloat16),
        "head",
        scatter_dimension=0,
    ).astype(jnp.float32)
    image_out = image_mid + per_request(image_mod[:, 5], image_mid, 0) * mlp[:, :image_tile]
    text_out = text_mid + per_request(text_mod[:, 5], text_mid, 0) * mlp[:, image_tile:]
    image_states = image_out.reshape(requests, tile_rows, tile_cols, model_width).astype(jnp.bfloat16)
    text_states = text_out.astype(jnp.bfloat16)
    final_in = modulate(image_out, final_mod[:, 1], final_mod[:, 0], 0).astype(jnp.bfloat16)
    velocity = jnp.einsum("rnd,dp->rnp", final_in, final_proj, preferred_element_type=jnp.float32)
    channels = velocity.shape[-1] // 4
    velocity = (
        velocity.reshape(requests, tile_rows, tile_cols, 2, 2, channels)
        .transpose(0, 1, 3, 2, 4, 5)
        .reshape(requests, 2 * tile_rows, 2 * tile_cols, channels)
    )
    current = step_index.astype(jnp.float32) / 1000.0
    following = jnp.maximum(step_index - 125, 0).astype(jnp.float32) / 1000.0
    step_size = noise_level(following) - noise_level(current)
    latent_next = latent_grid + step_size[:, None, None, None] * velocity
    decoded_in = (latent_next / 1.5305 + 0.0609).astype(jnp.bfloat16)
    padded = extended(decoded_in, (("head", 1), ("blk", 2)), 1)
    features = convolve(padded, conv_kernel)
    return (image_states, text_states, latent_next, features)


def solution(mesh):
    in_specs = (
        P("req", "head", "blk", None),
        P("req", ("head", "blk"), None),
        P("req", "head", "blk", None),
        P("req"),
        P("req"),
        P("req", None, None),
        P("req", None, None),
        P("req", None, None),
        P(),
        P(),
        P(None, None, "head"),
        P(None, None, "head"),
        P("head", None),
        P("head", None),
        P(None, "head"),
        P(None, "head"),
        P("head", None),
        P("head", None),
        P(),
        P(),
    )
    out_specs = (
        P("req", "head", "blk", None),
        P("req", ("head", "blk"), None),
        P("req", "head", "blk", None),
        P("req", "head", "blk", None),
    )
    return jax.shard_map(body, mesh=mesh, in_specs=in_specs, out_specs=out_specs, check_vma=False)
```

```python
import math

import jax
import jax.numpy as jnp
from jax import lax
from jax.sharding import PartitionSpec as P

HD = 64


def extended(block, sides, width):
    for axis, dim in sides:
        count = lax.axis_size(axis)
        forward = [(i, i + 1) for i in range(count - 1)]
        backward = [(target, source) for source, target in forward]
        low = lax.ppermute(
            lax.slice_in_dim(block, block.shape[dim] - width, None, axis=dim), axis, forward
        )
        high = lax.ppermute(lax.slice_in_dim(block, 0, width, axis=dim), axis, backward)
        block = jnp.concatenate([low, block, high], axis=dim)
    return block


def gather_slots(block, axis):
    count = lax.axis_size(axis)
    parts = [block]
    for shift in range(1, count):
        parts.append(lax.ppermute(block, axis, [(i, (i + shift) % count) for i in range(count)]))
    return jnp.stack(parts)


def scatter_slots(partial, axis):
    count = lax.axis_size(axis)
    total = partial[0].astype(jnp.float32)
    for shift in range(1, count):
        total = total + lax.ppermute(
            partial[shift], axis, [((i + shift) % count, i) for i in range(count)]
        ).astype(jnp.float32)
    return total


def per_request(vector, values, axis):
    shape = [1] * values.ndim
    shape[axis] = vector.shape[0]
    shape[-1] = vector.shape[-1]
    return vector.reshape(shape)


def modulate(values, shift, scale, axis):
    average = jnp.mean(values, -1, keepdims=True)
    centred = values - average
    spread = jnp.mean(centred * centred, -1, keepdims=True)
    normed = centred * lax.rsqrt(spread + 1e-06)
    return normed * (1.0 + per_request(scale, values, axis)) + per_request(shift, values, axis)


def head_norm(values, gain):
    shaped = values.reshape(values.shape[:-1] + (values.shape[-1] // HD, HD))
    return (shaped * lax.rsqrt(jnp.mean(shaped * shaped, -1, keepdims=True) + 1e-06) * gain).astype(
        jnp.bfloat16
    )


def noise_level(fraction):
    return 3.0 * fraction / (1.0 + 2.0 * fraction)


def attention_inputs(normed, weight, gains):
    projected = jnp.einsum("arnd,dje->arnje", normed, weight, preferred_element_type=jnp.float32)
    queries = head_norm(projected[..., 0, :], gains[0])
    key_heads = head_norm(projected[..., 1, :], gains[1])
    value_heads = projected[..., 2, :].reshape(queries.shape).astype(jnp.bfloat16)
    return (queries, key_heads, value_heads)


def convolve(padded, kernel):
    out_rows = padded.shape[1] - 2
    out_cols = padded.shape[2] - 2
    summed = jnp.zeros((padded.shape[0], out_rows, out_cols, kernel.shape[-1]), jnp.float32)
    for row_off in range(3):
        for col_off in range(3):
            summed = summed + jnp.einsum(
                "rhwc,co->rhwo",
                padded[:, row_off : row_off + out_rows, col_off : col_off + out_cols],
                kernel[row_off, col_off],
                preferred_element_type=jnp.float32,
            )
    return summed.astype(jnp.bfloat16)


def body(
    image_hidden,
    text_hidden,
    latent_grid,
    text_lengths,
    step_index,
    image_mod,
    text_mod,
    final_mod,
    image_qk_gain,
    text_qk_gain,
    image_qkv,
    text_qkv,
    image_proj,
    text_proj,
    image_up,
    text_up,
    image_down,
    text_down,
    final_proj,
    conv_kernel,
):
    blocks = lax.axis_size("blk")
    groups = lax.axis_size("head")
    requests, tile_rows, tile_cols, model_width = image_hidden.shape
    text_slice = text_hidden.shape[1]
    image_tile = tile_rows * tile_cols
    tile_tokens = image_tile + text_slice
    own = jnp.concatenate(
        [image_hidden.reshape(requests, image_tile, model_width), text_hidden], axis=1
    )
    strip = gather_slots(own, "head")
    strip_f = strip.astype(jnp.float32)
    image_x = strip_f[:, :, :image_tile]
    text_x = strip_f[:, :, image_tile:]
    image_norm = modulate(image_x, image_mod[:, 0], image_mod[:, 1], 1).astype(jnp.bfloat16)
    text_norm = modulate(text_x, text_mod[:, 0], text_mod[:, 1], 1).astype(jnp.bfloat16)
    image_q, image_k, image_v = attention_inputs(image_norm, image_qkv, image_qk_gain)
    text_q, text_k, text_v = attention_inputs(text_norm, text_qkv, text_qk_gain)
    queries = jnp.concatenate([image_q, text_q], 2)
    key_heads = jnp.concatenate([image_k, text_k], 2)
    value_heads = jnp.concatenate([image_v, text_v], 2)
    local_heads = queries.shape[3]
    score_scale = 1.0 / math.sqrt(HD)
    kv = gather_slots(jnp.stack([key_heads, value_heads]), "blk")
    span = blocks * groups * tile_tokens
    key_piece = kv[:, 0].transpose(2, 4, 0, 1, 3, 5).reshape(requests, local_heads, span, HD)
    value_piece = kv[:, 1].transpose(2, 4, 0, 1, 3, 5).reshape(requests, local_heads, span, HD)
    query_rows = groups * tile_tokens
    query_piece = queries.transpose(1, 3, 0, 2, 4).reshape(requests, local_heads, query_rows, HD)
    position = jnp.arange(span, dtype=jnp.int32)
    source = (lax.axis_index("blk") - position // (groups * tile_tokens)) % blocks
    group = (lax.axis_index("head") - (position // tile_tokens) % groups) % groups
    within = position % tile_tokens
    slot_ids = (group * blocks + source) * text_slice + (within - image_tile)
    usable = (within < image_tile)[None, :] | (slot_ids[None, :] < text_lengths[:, None])
    scores = (
        jnp.einsum("rhqd,rhkd->rhqk", query_piece, key_piece, preferred_element_type=jnp.float32)
        * score_scale
    )
    weights = jnp.exp(scores) * usable[:, None, None, :].astype(jnp.float32)
    denominator = jnp.sum(weights, -1)
    numerator = jnp.einsum(
        "rhqk,rhkd->rhqd",
        weights.astype(jnp.bfloat16),
        value_piece,
        preferred_element_type=jnp.float32,
    )
    context = (numerator / denominator[..., None]).astype(jnp.bfloat16)
    local_width = local_heads * HD
    context = (
        context.reshape(requests, local_heads, groups, tile_tokens, HD)
        .transpose(2, 0, 3, 1, 4)
        .reshape(groups, requests, tile_tokens, local_width)
    )
    image_part = jnp.einsum(
        "arne,ed->arnd", context[:, :, :image_tile], image_proj, preferred_element_type=jnp.float32
    )
    text_part = jnp.einsum(
        "arne,ed->arnd", context[:, :, image_tile:], text_proj, preferred_element_type=jnp.float32
    )
    attn = scatter_slots(jnp.concatenate([image_part, text_part], 2).astype(jnp.bfloat16), "head")
    own_f = own.astype(jnp.float32)
    image_mid = own_f[:, :image_tile] + per_request(image_mod[:, 2], own_f, 0) * attn[:, :image_tile]
    text_mid = own_f[:, image_tile:] + per_request(text_mod[:, 2], own_f, 0) * attn[:, image_tile:]
    image_local = modulate(image_mid, image_mod[:, 3], image_mod[:, 4], 0).astype(jnp.bfloat16)
    text_local = modulate(text_mid, text_mod[:, 3], text_mod[:, 4], 0).astype(jnp.bfloat16)
    ff_in = gather_slots(jnp.concatenate([image_local, text_local], 1), "head")
    image_hid = jax.nn.gelu(
        jnp.einsum("arnd,df->arnf", ff_in[:, :, :image_tile], image_up, preferred_element_type=jnp.float32),
        approximate=True,
    ).astype(jnp.bfloat16)
    text_hid = jax.nn.gelu(
        jnp.einsum("arnd,df->arnf", ff_in[:, :, image_tile:], text_up, preferred_element_type=jnp.float32),
        approximate=True,
    ).astype(jnp.bfloat16)
    image_back = jnp.einsum("arnf,fd->arnd", image_hid, image_down, preferred_element_type=jnp.float32)
    text_back = jnp.einsum("arnf,fd->arnd", text_hid, text_down, preferred_element_type=jnp.float32)
    mlp = scatter_slots(jnp.concatenate([image_back, text_back], 2).astype(jnp.bfloat16), "head")
    image_out = image_mid + per_request(image_mod[:, 5], image_mid, 0) * mlp[:, :image_tile]
    text_out = text_mid + per_request(text_mod[:, 5], text_mid, 0) * mlp[:, image_tile:]
    image_states = image_out.reshape(requests, tile_rows, tile_cols, model_width).astype(jnp.bfloat16)
    text_states = text_out.astype(jnp.bfloat16)
    final_in = modulate(image_out, final_mod[:, 1], final_mod[:, 0], 0).astype(jnp.bfloat16)
    velocity = jnp.einsum("rnd,dp->rnp", final_in, final_proj, preferred_element_type=jnp.float32)
    channels = velocity.shape[-1] // 4
    velocity = (
        velocity.reshape(requests, tile_rows, tile_cols, 2, 2, channels)
        .transpose(0, 1, 3, 2, 4, 5)
        .reshape(requests, 2 * tile_rows, 2 * tile_cols, channels)
    )
    current = step_index.astype(jnp.float32) / 1000.0
    following = jnp.maximum(step_index - 125, 0).astype(jnp.float32) / 1000.0
    step_size = noise_level(following) - noise_level(current)
    latent_next = latent_grid + step_size[:, None, None, None] * velocity
    decoded_in = (latent_next / 1.5305 + 0.0609).astype(jnp.bfloat16)
    padded = extended(decoded_in, (("head", 1), ("blk", 2)), 1)
    features = convolve(padded, conv_kernel)
    return (image_states, text_states, latent_next, features)


def solution(mesh):
    in_specs = (
        P("req", "head", "blk", None),
        P("req", ("head", "blk"), None),
        P("req", "head", "blk", None),
        P("req"),
        P("req"),
        P("req", None, None),
        P("req", None, None),
        P("req", None, None),
        P(),
        P(),
        P(None, None, "head"),
        P(None, None, "head"),
        P("head", None),
        P("head", None),
        P(None, "head"),
        P(None, "head"),
        P("head", None),
        P("head", None),
        P(),
        P(),
    )
    out_specs = (
        P("req", "head", "blk", None),
        P("req", ("head", "blk"), None),
        P("req", "head", "blk", None),
        P("req", "head", "blk", None),
    )
    return jax.shard_map(body, mesh=mesh, in_specs=in_specs, out_specs=out_specs, check_vma=False)
```

```python
import math

import jax
import jax.numpy as jnp
from jax import lax
from jax.sharding import PartitionSpec as P

HD = 64


def extended(block, sides, width):
    for axis, dim in sides:
        count = lax.axis_size(axis)
        forward = [(i, i + 1) for i in range(count - 1)]
        backward = [(target, source) for source, target in forward]
        low = lax.ppermute(
            lax.slice_in_dim(block, block.shape[dim] - width, None, axis=dim), axis, forward
        )
        high = lax.ppermute(lax.slice_in_dim(block, 0, width, axis=dim), axis, backward)
        block = jnp.concatenate([low, block, high], axis=dim)
    return block


def gather_slots(block, axis):
    count = lax.axis_size(axis)
    parts = [block]
    for shift in range(1, count):
        parts.append(lax.ppermute(block, axis, [(i, (i + shift) % count) for i in range(count)]))
    return jnp.stack(parts)


def scatter_slots(partial, axis):
    count = lax.axis_size(axis)
    total = partial[0].astype(jnp.float32)
    for shift in range(1, count):
        total = total + lax.ppermute(
            partial[shift], axis, [((i + shift) % count, i) for i in range(count)]
        ).astype(jnp.float32)
    return total


def per_request(vector, values, axis):
    shape = [1] * values.ndim
    shape[axis] = vector.shape[0]
    shape[-1] = vector.shape[-1]
    return vector.reshape(shape)


def modulate(values, shift, scale, axis):
    average = jnp.mean(values, -1, keepdims=True)
    centred = values - average
    spread = jnp.mean(centred * centred, -1, keepdims=True)
    normed = centred * lax.rsqrt(spread + 1e-06)
    return normed * (1.0 + per_request(scale, values, axis)) + per_request(shift, values, axis)


def head_norm(values, gain):
    width = values.shape[-1]
    lane_head = jnp.arange(width) // HD
    spread = (lane_head[:, None] == lane_head[None, :]).astype(jnp.float32) / HD
    mean_square = jnp.dot(values * values, spread, precision=lax.Precision.HIGHEST)
    return (values * lax.rsqrt(mean_square + 1e-06) * jnp.tile(gain, width // HD)).astype(jnp.bfloat16)


def noise_level(fraction):
    return 3.0 * fraction / (1.0 + 2.0 * fraction)


def attention_inputs(normed, weight, gains):
    projected = jnp.einsum("arnd,dje->arnje", normed, weight, preferred_element_type=jnp.float32)
    queries = head_norm(projected[..., 0, :], gains[0])
    key_heads = head_norm(projected[..., 1, :], gains[1])
    value_heads = projected[..., 2, :].astype(jnp.bfloat16)
    return (queries, key_heads, value_heads)


def convolve(padded, kernel):
    out_rows = padded.shape[1] - 2
    out_cols = padded.shape[2] - 2
    summed = jnp.zeros((padded.shape[0], out_rows, out_cols, kernel.shape[-1]), jnp.float32)
    for row_off in range(3):
        for col_off in range(3):
            summed = summed + jnp.einsum(
                "rhwc,co->rhwo",
                padded[:, row_off : row_off + out_rows, col_off : col_off + out_cols],
                kernel[row_off, col_off],
                preferred_element_type=jnp.float32,
            )
    return summed.astype(jnp.bfloat16)


def body(
    image_hidden,
    text_hidden,
    latent_grid,
    text_lengths,
    step_index,
    image_mod,
    text_mod,
    final_mod,
    image_qk_gain,
    text_qk_gain,
    image_qkv,
    text_qkv,
    image_proj,
    text_proj,
    image_up,
    text_up,
    image_down,
    text_down,
    final_proj,
    conv_kernel,
):
    blocks = lax.axis_size("blk")
    groups = lax.axis_size("head")
    requests, tile_rows, tile_cols, model_width = image_hidden.shape
    text_slice = text_hidden.shape[1]
    image_tile = tile_rows * tile_cols
    tile_tokens = image_tile + text_slice
    own = jnp.concatenate(
        [image_hidden.reshape(requests, image_tile, model_width), text_hidden], axis=1
    )
    strip = gather_slots(own, "head")
    strip_f = strip.astype(jnp.float32)
    image_x = strip_f[:, :, :image_tile]
    text_x = strip_f[:, :, image_tile:]
    image_norm = modulate(image_x, image_mod[:, 0], image_mod[:, 1], 1).astype(jnp.bfloat16)
    text_norm = modulate(text_x, text_mod[:, 0], text_mod[:, 1], 1).astype(jnp.bfloat16)
    image_q, image_k, image_v = attention_inputs(image_norm, image_qkv, image_qk_gain)
    text_q, text_k, text_v = attention_inputs(text_norm, text_qkv, text_qk_gain)
    queries = jnp.concatenate([image_q, text_q], 2)
    local_width = queries.shape[-1]
    local_heads = local_width // HD
    score_scale = 1.0 / math.sqrt(HD)
    key_value = jnp.concatenate(
        [jnp.concatenate([image_k, image_v], -1), jnp.concatenate([text_k, text_v], -1)], 2
    )
    kv = gather_slots(key_value.reshape(-1, 2 * local_width), "blk")
    span = blocks * groups * tile_tokens
    kv = kv.reshape(blocks, groups, requests, tile_tokens, 2, local_heads, HD)
    key_piece = kv[:, :, :, :, 0].transpose(2, 4, 0, 1, 3, 5).reshape(requests, local_heads, span, HD)
    value_piece = kv[:, :, :, :, 1].transpose(2, 4, 0, 1, 3, 5).reshape(requests, local_heads, span, HD)
    query_rows = groups * tile_tokens
    query_piece = (
        queries.reshape(groups, requests, tile_tokens, local_heads, HD)
        .transpose(1, 3, 0, 2, 4)
        .reshape(requests, local_heads, query_rows, HD)
    )
    position = jnp.arange(span, dtype=jnp.int32)
    source = (lax.axis_index("blk") - position // (groups * tile_tokens)) % blocks
    group = (lax.axis_index("head") - (position // tile_tokens) % groups) % groups
    within = position % tile_tokens
    slot_ids = (group * blocks + source) * text_slice + (within - image_tile)
    usable = (within < image_tile)[None, :] | (slot_ids[None, :] < text_lengths[:, None])
    scores = (
        jnp.einsum("rhqd,rhkd->rhqk", query_piece, key_piece, preferred_element_type=jnp.float32)
        * score_scale
    )
    weights = jnp.exp(scores) * usable[:, None, None, :].astype(jnp.float32)
    denominator = jnp.sum(weights, -1)
    numerator = jnp.einsum(
        "rhqk,rhkd->rhqd",
        weights.astype(jnp.bfloat16),
        value_piece,
        preferred_element_type=jnp.float32,
    )
    context = (numerator / denominator[..., None]).astype(jnp.bfloat16)
    context = (
        context.reshape(requests, local_heads, groups, tile_tokens, HD)
        .transpose(2, 0, 3, 1, 4)
        .reshape(groups, requests, tile_tokens, local_width)
    )
    image_part = jnp.einsum(
        "arne,ed->arnd", context[:, :, :image_tile], image_proj, preferred_element_type=jnp.float32
    )
    text_part = jnp.einsum(
        "arne,ed->arnd", context[:, :, image_tile:], text_proj, preferred_element_type=jnp.float32
    )
    attn = scatter_slots(jnp.concatenate([image_part, text_part], 2).astype(jnp.bfloat16), "head")
    own_f = own.astype(jnp.float32)
    image_mid = own_f[:, :image_tile] + per_request(image_mod[:, 2], own_f, 0) * attn[:, :image_tile]
    text_mid = own_f[:, image_tile:] + per_request(text_mod[:, 2], own_f, 0) * attn[:, image_tile:]
    image_local = modulate(image_mid, image_mod[:, 3], image_mod[:, 4], 0).astype(jnp.bfloat16)
    text_local = modulate(text_mid, text_mod[:, 3], text_mod[:, 4], 0).astype(jnp.bfloat16)
    ff_in = gather_slots(jnp.concatenate([image_local, text_local], 1), "head")
    image_hid = jax.nn.gelu(
        jnp.einsum("arnd,df->arnf", ff_in[:, :, :image_tile], image_up, preferred_element_type=jnp.float32),
        approximate=True,
    ).astype(jnp.bfloat16)
    text_hid = jax.nn.gelu(
        jnp.einsum("arnd,df->arnf", ff_in[:, :, image_tile:], text_up, preferred_element_type=jnp.float32),
        approximate=True,
    ).astype(jnp.bfloat16)
    image_back = jnp.einsum("arnf,fd->arnd", image_hid, image_down, preferred_element_type=jnp.float32)
    text_back = jnp.einsum("arnf,fd->arnd", text_hid, text_down, preferred_element_type=jnp.float32)
    mlp = scatter_slots(jnp.concatenate([image_back, text_back], 2).astype(jnp.bfloat16), "head")
    image_out = image_mid + per_request(image_mod[:, 5], image_mid, 0) * mlp[:, :image_tile]
    text_out = text_mid + per_request(text_mod[:, 5], text_mid, 0) * mlp[:, image_tile:]
    image_states = image_out.reshape(requests, tile_rows, tile_cols, model_width).astype(jnp.bfloat16)
    text_states = text_out.astype(jnp.bfloat16)
    final_in = modulate(image_out, final_mod[:, 1], final_mod[:, 0], 0).astype(jnp.bfloat16)
    velocity = jnp.einsum("rnd,dp->rnp", final_in, final_proj, preferred_element_type=jnp.float32)
    channels = velocity.shape[-1] // 4
    velocity = (
        velocity.reshape(requests, tile_rows, tile_cols, 2, 2, channels)
        .transpose(0, 1, 3, 2, 4, 5)
        .reshape(requests, 2 * tile_rows, 2 * tile_cols, channels)
    )
    current = step_index.astype(jnp.float32) / 1000.0
    following = jnp.maximum(step_index - 125, 0).astype(jnp.float32) / 1000.0
    step_size = noise_level(following) - noise_level(current)
    latent_next = latent_grid + step_size[:, None, None, None] * velocity
    decoded_in = (latent_next / 1.5305 + 0.0609).astype(jnp.bfloat16)
    padded = extended(decoded_in, (("head", 1), ("blk", 2)), 1)
    features = convolve(padded, conv_kernel)
    return (image_states, text_states, latent_next, features)


def solution(mesh):
    in_specs = (
        P("req", "head", "blk", None),
        P("req", ("head", "blk"), None),
        P("req", "head", "blk", None),
        P("req"),
        P("req"),
        P("req", None, None),
        P("req", None, None),
        P("req", None, None),
        P(),
        P(),
        P(None, None, "head"),
        P(None, None, "head"),
        P("head", None),
        P("head", None),
        P(None, "head"),
        P(None, "head"),
        P("head", None),
        P("head", None),
        P(),
        P(),
    )
    out_specs = (
        P("req", "head", "blk", None),
        P("req", ("head", "blk"), None),
        P("req", "head", "blk", None),
        P("req", "head", "blk", None),
    )
    return jax.shard_map(body, mesh=mesh, in_specs=in_specs, out_specs=out_specs, check_vma=False)
```

```python
import math

import jax
import jax.numpy as jnp
from jax import lax
from jax.sharding import PartitionSpec as P

HD = 64


def extended(block, sides, width):
    for axis, dim in sides:
        count = lax.axis_size(axis)
        forward = [(i, i + 1) for i in range(count - 1)]
        backward = [(target, source) for source, target in forward]
        low = lax.ppermute(
            lax.slice_in_dim(block, block.shape[dim] - width, None, axis=dim), axis, forward
        )
        high = lax.ppermute(lax.slice_in_dim(block, 0, width, axis=dim), axis, backward)
        block = jnp.concatenate([low, block, high], axis=dim)
    return block


def per_request(vector, values, axis):
    shape = [1] * values.ndim
    shape[axis] = vector.shape[0]
    shape[-1] = vector.shape[-1]
    return vector.reshape(shape)


def modulate(values, shift, scale, axis):
    average = jnp.mean(values, -1, keepdims=True)
    centred = values - average
    spread = jnp.mean(centred * centred, -1, keepdims=True)
    normed = centred * lax.rsqrt(spread + 1e-06)
    return normed * (1.0 + per_request(scale, values, axis)) + per_request(shift, values, axis)


def head_norm(values, gain):
    width = values.shape[-1]
    lane_head = jnp.arange(width) // HD
    spread = (lane_head[:, None] == lane_head[None, :]).astype(jnp.float32) / HD
    mean_square = jnp.dot(values * values, spread, precision=lax.Precision.HIGHEST)
    return (values * lax.rsqrt(mean_square + 1e-06) * jnp.tile(gain, width // HD)).astype(jnp.bfloat16)


def noise_level(fraction):
    return 3.0 * fraction / (1.0 + 2.0 * fraction)


def attention_inputs(normed, weight, gains):
    projected = jnp.einsum("arnd,dje->arnje", normed, weight, preferred_element_type=jnp.float32)
    queries = head_norm(projected[..., 0, :], gains[0])
    key_heads = head_norm(projected[..., 1, :], gains[1])
    value_heads = projected[..., 2, :].astype(jnp.bfloat16)
    return (queries, key_heads, value_heads)


def convolve(padded, kernel):
    out_rows = padded.shape[1] - 2
    out_cols = padded.shape[2] - 2
    summed = jnp.zeros((padded.shape[0], out_rows, out_cols, kernel.shape[-1]), jnp.float32)
    for row_off in range(3):
        for col_off in range(3):
            summed = summed + jnp.einsum(
                "rhwc,co->rhwo",
                padded[:, row_off : row_off + out_rows, col_off : col_off + out_cols],
                kernel[row_off, col_off],
                preferred_element_type=jnp.float32,
            )
    return summed.astype(jnp.bfloat16)


def send_slots(block, axis):
    count = lax.axis_size(axis)
    parts = [block]
    for shift in range(1, count):
        parts.append(lax.ppermute(block, axis, [(i, (i + shift) % count) for i in range(count)]))
    return parts


def return_slots(parts, axis):
    count = lax.axis_size(axis)
    total = parts[0].astype(jnp.float32)
    for shift in range(1, count):
        total = total + lax.ppermute(
            parts[shift], axis, [((i + shift) % count, i) for i in range(count)]
        ).astype(jnp.float32)
    return total


def attend(query_piece, key_value, usable, local_heads):
    requests, keys, _ = key_value.shape
    shaped = key_value.reshape(requests, keys, 2, local_heads, HD)
    key_piece = shaped[:, :, 0]
    value_piece = shaped[:, :, 1]
    scores = jnp.einsum(
        "rhqd,rkhd->rhqk", query_piece, key_piece, preferred_element_type=jnp.float32
    ) * (1.0 / math.sqrt(HD))
    weights = jnp.exp(scores) * usable[:, None, None, :].astype(jnp.float32)
    denominator = jnp.sum(weights, -1)
    numerator = jnp.einsum(
        "rhqk,rkhd->rhqd", weights.astype(jnp.bfloat16), value_piece, preferred_element_type=jnp.float32
    )
    return numerator, denominator


def body(
    image_hidden,
    text_hidden,
    latent_grid,
    text_lengths,
    step_index,
    image_mod,
    text_mod,
    final_mod,
    image_qk_gain,
    text_qk_gain,
    image_qkv,
    text_qkv,
    image_proj,
    text_proj,
    image_up,
    text_up,
    image_down,
    text_down,
    final_proj,
    conv_kernel,
):
    blocks = lax.axis_size("blk")
    groups = lax.axis_size("head")
    requests, tile_rows, tile_cols, model_width = image_hidden.shape
    text_slice = text_hidden.shape[1]
    image_tile = tile_rows * tile_cols
    tile_tokens = image_tile + text_slice
    own = jnp.concatenate(
        [image_hidden.reshape(requests, image_tile, model_width), text_hidden], axis=1
    )
    query_slots = []
    kv_slots = []
    for block in send_slots(own, "head"):
        values = block.astype(jnp.float32)
        image_norm = modulate(values[:, :image_tile], image_mod[:, 0], image_mod[:, 1], 0)
        text_norm = modulate(values[:, image_tile:], text_mod[:, 0], text_mod[:, 1], 0)
        image_q, image_k, image_v = attention_inputs(
            image_norm.astype(jnp.bfloat16)[None], image_qkv, image_qk_gain
        )
        text_q, text_k, text_v = attention_inputs(
            text_norm.astype(jnp.bfloat16)[None], text_qkv, text_qk_gain
        )
        query_slots.append(jnp.concatenate([image_q[0], text_q[0]], 1))
        kv_slots.append(
            jnp.concatenate(
                [jnp.concatenate([image_k[0], image_v[0]], -1), jnp.concatenate([text_k[0], text_v[0]], -1)],
                1,
            )
        )
    local_width = query_slots[0].shape[-1]
    local_heads = local_width // HD
    key_value = jnp.stack(kv_slots)
    kv_blocks = send_slots(key_value.reshape(-1, 2 * local_width), "blk")
    query_rows = groups * tile_tokens
    query_piece = (
        jnp.stack(query_slots)
        .reshape(groups, requests, tile_tokens, local_heads, HD)
        .transpose(1, 3, 0, 2, 4)
        .reshape(requests, local_heads, query_rows, HD)
    )
    position = jnp.arange(query_rows, dtype=jnp.int32)
    group = (lax.axis_index("head") - position // tile_tokens) % groups
    within = position % tile_tokens
    numerator = None
    denominator = None
    for shift, kv_block in enumerate(kv_blocks):
        source = (lax.axis_index("blk") - shift) % blocks
        slot_ids = (group * blocks + source) * text_slice + (within - image_tile)
        usable = (within < image_tile)[None, :] | (slot_ids[None, :] < text_lengths[:, None])
        block_kv = (
            kv_block.reshape(groups, requests, tile_tokens, 2 * local_width)
            .transpose(1, 0, 2, 3)
            .reshape(requests, query_rows, 2 * local_width)
        )
        part_num, part_den = attend(query_piece, block_kv, usable, local_heads)
        numerator = part_num if numerator is None else numerator + part_num
        denominator = part_den if denominator is None else denominator + part_den
    context = (numerator / denominator[..., None]).astype(jnp.bfloat16)
    context = (
        context.reshape(requests, local_heads, groups, tile_tokens, HD)
        .transpose(2, 0, 3, 1, 4)
        .reshape(groups, requests, tile_tokens, local_width)
    )
    attn_parts = []
    for slot in range(groups):
        image_part = jnp.einsum(
            "rne,ed->rnd", context[slot, :, :image_tile], image_proj, preferred_element_type=jnp.float32
        )
        text_part = jnp.einsum(
            "rne,ed->rnd", context[slot, :, image_tile:], text_proj, preferred_element_type=jnp.float32
        )
        attn_parts.append(jnp.concatenate([image_part, text_part], 1).astype(jnp.bfloat16))
    attn = return_slots(attn_parts, "head")
    own_f = own.astype(jnp.float32)
    image_mid = own_f[:, :image_tile] + per_request(image_mod[:, 2], own_f, 0) * attn[:, :image_tile]
    text_mid = own_f[:, image_tile:] + per_request(text_mod[:, 2], own_f, 0) * attn[:, image_tile:]
    image_local = modulate(image_mid, image_mod[:, 3], image_mod[:, 4], 0).astype(jnp.bfloat16)
    text_local = modulate(text_mid, text_mod[:, 3], text_mod[:, 4], 0).astype(jnp.bfloat16)
    ff_parts = []
    for block in send_slots(jnp.concatenate([image_local, text_local], 1), "head"):
        image_hid = jax.nn.gelu(
            jnp.einsum("rnd,df->rnf", block[:, :image_tile], image_up, preferred_element_type=jnp.float32),
            approximate=True,
        ).astype(jnp.bfloat16)
        text_hid = jax.nn.gelu(
            jnp.einsum("rnd,df->rnf", block[:, image_tile:], text_up, preferred_element_type=jnp.float32),
            approximate=True,
        ).astype(jnp.bfloat16)
        image_back = jnp.einsum("rnf,fd->rnd", image_hid, image_down, preferred_element_type=jnp.float32)
        text_back = jnp.einsum("rnf,fd->rnd", text_hid, text_down, preferred_element_type=jnp.float32)
        ff_parts.append(jnp.concatenate([image_back, text_back], 1).astype(jnp.bfloat16))
    mlp = return_slots(ff_parts, "head")
    image_out = image_mid + per_request(image_mod[:, 5], image_mid, 0) * mlp[:, :image_tile]
    text_out = text_mid + per_request(text_mod[:, 5], text_mid, 0) * mlp[:, image_tile:]
    image_states = image_out.reshape(requests, tile_rows, tile_cols, model_width).astype(jnp.bfloat16)
    text_states = text_out.astype(jnp.bfloat16)
    final_in = modulate(image_out, final_mod[:, 1], final_mod[:, 0], 0).astype(jnp.bfloat16)
    velocity = jnp.einsum("rnd,dp->rnp", final_in, final_proj, preferred_element_type=jnp.float32)
    channels = velocity.shape[-1] // 4
    velocity = (
        velocity.reshape(requests, tile_rows, tile_cols, 2, 2, channels)
        .transpose(0, 1, 3, 2, 4, 5)
        .reshape(requests, 2 * tile_rows, 2 * tile_cols, channels)
    )
    current = step_index.astype(jnp.float32) / 1000.0
    following = jnp.maximum(step_index - 125, 0).astype(jnp.float32) / 1000.0
    step_size = noise_level(following) - noise_level(current)
    latent_next = latent_grid + step_size[:, None, None, None] * velocity
    decoded_in = (latent_next / 1.5305 + 0.0609).astype(jnp.bfloat16)
    padded = extended(decoded_in, (("head", 1), ("blk", 2)), 1)
    features = convolve(padded, conv_kernel)
    return (image_states, text_states, latent_next, features)


def solution(mesh):
    in_specs = (
        P("req", "head", "blk", None),
        P("req", ("head", "blk"), None),
        P("req", "head", "blk", None),
        P("req"),
        P("req"),
        P("req", None, None),
        P("req", None, None),
        P("req", None, None),
        P(),
        P(),
        P(None, None, "head"),
        P(None, None, "head"),
        P("head", None),
        P("head", None),
        P(None, "head"),
        P(None, "head"),
        P("head", None),
        P("head", None),
        P(),
        P(),
    )
    out_specs = (
        P("req", "head", "blk", None),
        P("req", ("head", "blk"), None),
        P("req", "head", "blk", None),
        P("req", "head", "blk", None),
    )
    return jax.shard_map(body, mesh=mesh, in_specs=in_specs, out_specs=out_specs, check_vma=False)
```

```python
import math

import jax
import jax.numpy as jnp
from jax import lax
from jax.sharding import PartitionSpec as P

HD = 64


def extended(block, sides, width):
    for axis, dim in sides:
        count = lax.axis_size(axis)
        forward = [(i, i + 1) for i in range(count - 1)]
        backward = [(target, source) for source, target in forward]
        low = lax.ppermute(
            lax.slice_in_dim(block, block.shape[dim] - width, None, axis=dim), axis, forward
        )
        high = lax.ppermute(lax.slice_in_dim(block, 0, width, axis=dim), axis, backward)
        block = jnp.concatenate([low, block, high], axis=dim)
    return block


def gather_slots(block, axis):
    count = lax.axis_size(axis)
    parts = [block]
    for shift in range(1, count):
        parts.append(lax.ppermute(block, axis, [(i, (i + shift) % count) for i in range(count)]))
    return jnp.stack(parts)


def scatter_slots(partial, axis):
    count = lax.axis_size(axis)
    total = partial[0].astype(jnp.float32)
    for shift in range(1, count):
        total = total + lax.ppermute(
            partial[shift], axis, [((i + shift) % count, i) for i in range(count)]
        ).astype(jnp.float32)
    return total


def per_request(vector, values, axis):
    shape = [1] * values.ndim
    shape[axis] = vector.shape[0]
    shape[-1] = vector.shape[-1]
    return vector.reshape(shape)


def modulate(values, shift, scale, axis):
    average = jnp.mean(values, -1, keepdims=True)
    centred = values - average
    spread = jnp.mean(centred * centred, -1, keepdims=True)
    normed = centred * lax.rsqrt(spread + 1e-06)
    return normed * (1.0 + per_request(scale, values, axis)) + per_request(shift, values, axis)


def head_norm(values, gain):
    width = values.shape[-1]
    lane_head = jnp.arange(width) // HD
    spread = (lane_head[:, None] == lane_head[None, :]).astype(jnp.float32) / HD
    mean_square = jnp.dot(values * values, spread, precision=lax.Precision.HIGHEST)
    return (values * lax.rsqrt(mean_square + 1e-06) * jnp.tile(gain, width // HD)).astype(jnp.bfloat16)


def noise_level(fraction):
    return 3.0 * fraction / (1.0 + 2.0 * fraction)


def attention_inputs(normed, weight, gains):
    model_width, _, local_width = weight.shape
    heads = local_width // HD
    split = weight.reshape(model_width, 3, heads, HD)
    query_weight = jnp.concatenate([split[:, 0], jnp.zeros_like(split[:, 0])], -1).reshape(
        model_width, 2 * local_width
    )
    pair_weight = jnp.concatenate([split[:, 1], split[:, 2]], -1).reshape(model_width, 2 * local_width)
    lane = jnp.arange(2 * local_width)
    live = (lane % (2 * HD)) < HD
    lane_head = lane // (2 * HD)
    spread = ((lane_head[:, None] == lane_head[None, :]) & live[:, None]).astype(jnp.float32) / HD
    query_gain = jnp.where(live, jnp.tile(jnp.concatenate([gains[0], gains[0]]), heads), 0.0)
    key_gain = jnp.tile(jnp.concatenate([gains[1], gains[1]]), heads)

    def normalized(values, gain):
        mean_square = jnp.dot(values * values, spread, precision=lax.Precision.HIGHEST)
        return values * lax.rsqrt(mean_square + 1e-06) * gain

    query_proj = jnp.einsum("arnd,de->arne", normed, query_weight, preferred_element_type=jnp.float32)
    pair_proj = jnp.einsum("arnd,de->arne", normed, pair_weight, preferred_element_type=jnp.float32)
    queries = normalized(query_proj, query_gain).astype(jnp.bfloat16)
    pairs = jnp.where(live, normalized(pair_proj, key_gain), pair_proj).astype(jnp.bfloat16)
    return queries, pairs


def convolve(padded, kernel):
    out_rows = padded.shape[1] - 2
    out_cols = padded.shape[2] - 2
    summed = jnp.zeros((padded.shape[0], out_rows, out_cols, kernel.shape[-1]), jnp.float32)
    for row_off in range(3):
        for col_off in range(3):
            summed = summed + jnp.einsum(
                "rhwc,co->rhwo",
                padded[:, row_off : row_off + out_rows, col_off : col_off + out_cols],
                kernel[row_off, col_off],
                preferred_element_type=jnp.float32,
            )
    return summed.astype(jnp.bfloat16)


def body(
    image_hidden,
    text_hidden,
    latent_grid,
    text_lengths,
    step_index,
    image_mod,
    text_mod,
    final_mod,
    image_qk_gain,
    text_qk_gain,
    image_qkv,
    text_qkv,
    image_proj,
    text_proj,
    image_up,
    text_up,
    image_down,
    text_down,
    final_proj,
    conv_kernel,
):
    blocks = lax.axis_size("blk")
    groups = lax.axis_size("head")
    requests, tile_rows, tile_cols, model_width = image_hidden.shape
    text_slice = text_hidden.shape[1]
    image_tile = tile_rows * tile_cols
    tile_tokens = image_tile + text_slice
    own = jnp.concatenate(
        [image_hidden.reshape(requests, image_tile, model_width), text_hidden], axis=1
    )
    strip = gather_slots(own, "head")
    strip_f = strip.astype(jnp.float32)
    image_x = strip_f[:, :, :image_tile]
    text_x = strip_f[:, :, image_tile:]
    image_norm = modulate(image_x, image_mod[:, 0], image_mod[:, 1], 1).astype(jnp.bfloat16)
    text_norm = modulate(text_x, text_mod[:, 0], text_mod[:, 1], 1).astype(jnp.bfloat16)
    image_q, image_kv = attention_inputs(image_norm, image_qkv, image_qk_gain)
    text_q, text_kv = attention_inputs(text_norm, text_qkv, text_qk_gain)
    queries = jnp.concatenate([image_q, text_q], 2)
    key_value = jnp.concatenate([image_kv, text_kv], 2)
    tile = 2 * HD
    local_heads = queries.shape[-1] // tile
    local_width = local_heads * HD
    score_scale = 1.0 / math.sqrt(HD)
    kv = gather_slots(key_value.reshape(-1, local_heads * tile), "blk")
    span = blocks * groups * tile_tokens
    key_piece = (
        kv.reshape(blocks, groups, requests, tile_tokens, local_heads, tile)
        .transpose(2, 4, 0, 1, 3, 5)
        .reshape(requests, local_heads, span, tile)
    )
    query_rows = groups * tile_tokens
    query_piece = (
        queries.reshape(groups, requests, tile_tokens, local_heads, tile)
        .transpose(1, 3, 0, 2, 4)
        .reshape(requests, local_heads, query_rows, tile)
    )
    position = jnp.arange(span, dtype=jnp.int32)
    source = (lax.axis_index("blk") - position // (groups * tile_tokens)) % blocks
    group = (lax.axis_index("head") - (position // tile_tokens) % groups) % groups
    within = position % tile_tokens
    slot_ids = (group * blocks + source) * text_slice + (within - image_tile)
    usable = (within < image_tile)[None, :] | (slot_ids[None, :] < text_lengths[:, None])
    scores = (
        jnp.einsum("rhqe,rhke->rhqk", query_piece, key_piece, preferred_element_type=jnp.float32)
        * score_scale
    )
    weights = jnp.exp(scores) * usable[:, None, None, :].astype(jnp.float32)
    denominator = jnp.sum(weights, -1)
    numerator = jnp.einsum(
        "rhqk,rhke->rhqe",
        weights.astype(jnp.bfloat16),
        key_piece,
        preferred_element_type=jnp.float32,
    )[..., HD:]
    context = (numerator / denominator[..., None]).astype(jnp.bfloat16)
    context = (
        context.reshape(requests, local_heads, groups, tile_tokens, HD)
        .transpose(2, 0, 3, 1, 4)
        .reshape(groups, requests, tile_tokens, local_width)
    )
    image_part = jnp.einsum(
        "arne,ed->arnd", context[:, :, :image_tile], image_proj, preferred_element_type=jnp.float32
    )
    text_part = jnp.einsum(
        "arne,ed->arnd", context[:, :, image_tile:], text_proj, preferred_element_type=jnp.float32
    )
    attn = scatter_slots(jnp.concatenate([image_part, text_part], 2).astype(jnp.bfloat16), "head")
    own_f = own.astype(jnp.float32)
    image_mid = own_f[:, :image_tile] + per_request(image_mod[:, 2], own_f, 0) * attn[:, :image_tile]
    text_mid = own_f[:, image_tile:] + per_request(text_mod[:, 2], own_f, 0) * attn[:, image_tile:]
    image_local = modulate(image_mid, image_mod[:, 3], image_mod[:, 4], 0).astype(jnp.bfloat16)
    text_local = modulate(text_mid, text_mod[:, 3], text_mod[:, 4], 0).astype(jnp.bfloat16)
    ff_in = gather_slots(jnp.concatenate([image_local, text_local], 1), "head")
    image_hid = jax.nn.gelu(
        jnp.einsum("arnd,df->arnf", ff_in[:, :, :image_tile], image_up, preferred_element_type=jnp.float32),
        approximate=True,
    ).astype(jnp.bfloat16)
    text_hid = jax.nn.gelu(
        jnp.einsum("arnd,df->arnf", ff_in[:, :, image_tile:], text_up, preferred_element_type=jnp.float32),
        approximate=True,
    ).astype(jnp.bfloat16)
    image_back = jnp.einsum("arnf,fd->arnd", image_hid, image_down, preferred_element_type=jnp.float32)
    text_back = jnp.einsum("arnf,fd->arnd", text_hid, text_down, preferred_element_type=jnp.float32)
    mlp = scatter_slots(jnp.concatenate([image_back, text_back], 2).astype(jnp.bfloat16), "head")
    image_out = image_mid + per_request(image_mod[:, 5], image_mid, 0) * mlp[:, :image_tile]
    text_out = text_mid + per_request(text_mod[:, 5], text_mid, 0) * mlp[:, image_tile:]
    image_states = image_out.reshape(requests, tile_rows, tile_cols, model_width).astype(jnp.bfloat16)
    text_states = text_out.astype(jnp.bfloat16)
    final_in = modulate(image_out, final_mod[:, 1], final_mod[:, 0], 0).astype(jnp.bfloat16)
    velocity = jnp.einsum("rnd,dp->rnp", final_in, final_proj, preferred_element_type=jnp.float32)
    channels = velocity.shape[-1] // 4
    velocity = (
        velocity.reshape(requests, tile_rows, tile_cols, 2, 2, channels)
        .transpose(0, 1, 3, 2, 4, 5)
        .reshape(requests, 2 * tile_rows, 2 * tile_cols, channels)
    )
    current = step_index.astype(jnp.float32) / 1000.0
    following = jnp.maximum(step_index - 125, 0).astype(jnp.float32) / 1000.0
    step_size = noise_level(following) - noise_level(current)
    latent_next = latent_grid + step_size[:, None, None, None] * velocity
    decoded_in = (latent_next / 1.5305 + 0.0609).astype(jnp.bfloat16)
    padded = extended(decoded_in, (("head", 1), ("blk", 2)), 1)
    features = convolve(padded, conv_kernel)
    return (image_states, text_states, latent_next, features)


def solution(mesh):
    in_specs = (
        P("req", "head", "blk", None),
        P("req", ("head", "blk"), None),
        P("req", "head", "blk", None),
        P("req"),
        P("req"),
        P("req", None, None),
        P("req", None, None),
        P("req", None, None),
        P(),
        P(),
        P(None, None, "head"),
        P(None, None, "head"),
        P("head", None),
        P("head", None),
        P(None, "head"),
        P(None, "head"),
        P("head", None),
        P("head", None),
        P(),
        P(),
    )
    out_specs = (
        P("req", "head", "blk", None),
        P("req", ("head", "blk"), None),
        P("req", "head", "blk", None),
        P("req", "head", "blk", None),
    )
    return jax.shard_map(body, mesh=mesh, in_specs=in_specs, out_specs=out_specs, check_vma=False)
```

```python
import math

import jax
import jax.numpy as jnp
from jax import lax
from jax.sharding import PartitionSpec as P

HD = 64


def extended(block, sides, width):
    for axis, dim in sides:
        count = lax.axis_size(axis)
        forward = [(i, i + 1) for i in range(count - 1)]
        backward = [(target, source) for source, target in forward]
        low = lax.ppermute(
            lax.slice_in_dim(block, block.shape[dim] - width, None, axis=dim), axis, forward
        )
        high = lax.ppermute(lax.slice_in_dim(block, 0, width, axis=dim), axis, backward)
        block = jnp.concatenate([low, block, high], axis=dim)
    return block


def gather_slots(block, axis):
    count = lax.axis_size(axis)
    parts = [block]
    for shift in range(1, count):
        parts.append(lax.ppermute(block, axis, [(i, (i + shift) % count) for i in range(count)]))
    return jnp.stack(parts)


def scatter_slots(partial, axis):
    count = lax.axis_size(axis)
    total = partial[0].astype(jnp.float32)
    for shift in range(1, count):
        total = total + lax.ppermute(
            partial[shift], axis, [((i + shift) % count, i) for i in range(count)]
        ).astype(jnp.float32)
    return total


def per_request(vector, values, axis):
    shape = [1] * values.ndim
    shape[axis] = vector.shape[0]
    shape[-1] = vector.shape[-1]
    return vector.reshape(shape)


def modulate(values, shift, scale, axis):
    average = jnp.mean(values, -1, keepdims=True)
    centred = values - average
    spread = jnp.mean(centred * centred, -1, keepdims=True)
    normed = centred * lax.rsqrt(spread + 1e-06)
    return normed * (1.0 + per_request(scale, values, axis)) + per_request(shift, values, axis)


def head_norm(values, gain):
    width = values.shape[-1]
    lane_head = jnp.arange(width) // HD
    spread = (lane_head[:, None] == lane_head[None, :]).astype(jnp.float32) / HD
    mean_square = jnp.dot(values * values, spread, precision=lax.Precision.HIGHEST)
    return (values * lax.rsqrt(mean_square + 1e-06) * jnp.tile(gain, width // HD)).astype(jnp.bfloat16)


def noise_level(fraction):
    return 3.0 * fraction / (1.0 + 2.0 * fraction)


def attention_inputs(normed, weight, gains):
    model_width, _, local_width = weight.shape
    heads = local_width // HD
    split = weight.reshape(model_width, 3, heads, HD)
    query_weight = jnp.concatenate([split[:, 0], jnp.zeros_like(split[:, 0])], -1).reshape(
        model_width, 2 * local_width
    )
    pair_weight = jnp.concatenate([split[:, 1], split[:, 2]], -1).reshape(model_width, 2 * local_width)
    lane = jnp.arange(2 * local_width)
    live = (lane % (2 * HD)) < HD
    lane_head = lane // (2 * HD)
    spread = ((lane_head[:, None] == lane_head[None, :]) & live[:, None]).astype(jnp.float32) / HD
    query_gain = jnp.where(live, jnp.tile(jnp.concatenate([gains[0], gains[0]]), heads), 0.0)
    key_gain = jnp.tile(jnp.concatenate([gains[1], gains[1]]), heads)

    def normalized(values, gain):
        mean_square = jnp.dot(values * values, spread, precision=lax.Precision.HIGHEST)
        return values * lax.rsqrt(mean_square + 1e-06) * gain

    query_proj = jnp.einsum("arnd,de->arne", normed, query_weight, preferred_element_type=jnp.float32)
    pair_proj = jnp.einsum("arnd,de->arne", normed, pair_weight, preferred_element_type=jnp.float32)
    queries = normalized(query_proj, query_gain).astype(jnp.bfloat16)
    pairs = jnp.where(live, normalized(pair_proj, key_gain), pair_proj).astype(jnp.bfloat16)
    return queries, pairs


def convolve(padded, kernel):
    out_rows = padded.shape[1] - 2
    out_cols = padded.shape[2] - 2
    summed = jnp.zeros((padded.shape[0], out_rows, out_cols, kernel.shape[-1]), jnp.float32)
    for row_off in range(3):
        for col_off in range(3):
            summed = summed + jnp.einsum(
                "rhwc,co->rhwo",
                padded[:, row_off : row_off + out_rows, col_off : col_off + out_cols],
                kernel[row_off, col_off],
                preferred_element_type=jnp.float32,
            )
    return summed.astype(jnp.bfloat16)


def layer(image_hidden, text_hidden, text_lengths, image_mod, text_mod, image_qk_gain, text_qk_gain,
          image_qkv, text_qkv, image_proj, text_proj, image_up, text_up, image_down, text_down):
    blocks = lax.axis_size("blk")
    groups = lax.axis_size("head")
    requests, tile_rows, tile_cols, model_width = image_hidden.shape
    text_slice = text_hidden.shape[1]
    image_tile = tile_rows * tile_cols
    tile_tokens = image_tile + text_slice
    own = jnp.concatenate(
        [image_hidden.reshape(requests, image_tile, model_width), text_hidden], axis=1
    )
    strip = gather_slots(own, "head")
    strip_f = strip.astype(jnp.float32)
    image_x = strip_f[:, :, :image_tile]
    text_x = strip_f[:, :, image_tile:]
    image_norm = modulate(image_x, image_mod[:, 0], image_mod[:, 1], 1).astype(jnp.bfloat16)
    text_norm = modulate(text_x, text_mod[:, 0], text_mod[:, 1], 1).astype(jnp.bfloat16)
    image_q, image_kv = attention_inputs(image_norm, image_qkv, image_qk_gain)
    text_q, text_kv = attention_inputs(text_norm, text_qkv, text_qk_gain)
    queries = jnp.concatenate([image_q, text_q], 2)
    key_value = jnp.concatenate([image_kv, text_kv], 2)
    tile = 2 * HD
    local_heads = queries.shape[-1] // tile
    local_width = local_heads * HD
    score_scale = 1.0 / math.sqrt(HD)
    kv = gather_slots(key_value.reshape(-1, local_heads * tile), "blk")
    span = blocks * groups * tile_tokens
    key_piece = (
        kv.reshape(blocks, groups, requests, tile_tokens, local_heads, tile)
        .transpose(2, 4, 0, 1, 3, 5)
        .reshape(requests, local_heads, span, tile)
    )
    query_rows = groups * tile_tokens
    query_piece = (
        queries.reshape(groups, requests, tile_tokens, local_heads, tile)
        .transpose(1, 3, 0, 2, 4)
        .reshape(requests, local_heads, query_rows, tile)
    )
    position = jnp.arange(span, dtype=jnp.int32)
    source = (lax.axis_index("blk") - position // (groups * tile_tokens)) % blocks
    group = (lax.axis_index("head") - (position // tile_tokens) % groups) % groups
    within = position % tile_tokens
    slot_ids = (group * blocks + source) * text_slice + (within - image_tile)
    usable = (within < image_tile)[None, :] | (slot_ids[None, :] < text_lengths[:, None])
    scores = (
        jnp.einsum("rhqe,rhke->rhqk", query_piece, key_piece, preferred_element_type=jnp.float32)
        * score_scale
    )
    weights = jnp.exp(scores) * usable[:, None, None, :].astype(jnp.float32)
    denominator = jnp.sum(weights, -1)
    numerator = jnp.einsum(
        "rhqk,rhke->rhqe",
        weights.astype(jnp.bfloat16),
        key_piece,
        preferred_element_type=jnp.float32,
    )[..., HD:]
    context = (numerator / denominator[..., None]).astype(jnp.bfloat16)
    context = (
        context.reshape(requests, local_heads, groups, tile_tokens, HD)
        .transpose(2, 0, 3, 1, 4)
        .reshape(groups, requests, tile_tokens, local_width)
    )
    image_part = jnp.einsum(
        "arne,ed->arnd", context[:, :, :image_tile], image_proj, preferred_element_type=jnp.float32
    )
    text_part = jnp.einsum(
        "arne,ed->arnd", context[:, :, image_tile:], text_proj, preferred_element_type=jnp.float32
    )
    attn = scatter_slots(jnp.concatenate([image_part, text_part], 2).astype(jnp.bfloat16), "head")
    own_f = own.astype(jnp.float32)
    image_mid = own_f[:, :image_tile] + per_request(image_mod[:, 2], own_f, 0) * attn[:, :image_tile]
    text_mid = own_f[:, image_tile:] + per_request(text_mod[:, 2], own_f, 0) * attn[:, image_tile:]
    image_local = modulate(image_mid, image_mod[:, 3], image_mod[:, 4], 0).astype(jnp.bfloat16)
    text_local = modulate(text_mid, text_mod[:, 3], text_mod[:, 4], 0).astype(jnp.bfloat16)
    ff_in = gather_slots(jnp.concatenate([image_local, text_local], 1), "head")
    image_hid = jax.nn.gelu(
        jnp.einsum("arnd,df->arnf", ff_in[:, :, :image_tile], image_up, preferred_element_type=jnp.float32),
        approximate=True,
    ).astype(jnp.bfloat16)
    text_hid = jax.nn.gelu(
        jnp.einsum("arnd,df->arnf", ff_in[:, :, image_tile:], text_up, preferred_element_type=jnp.float32),
        approximate=True,
    ).astype(jnp.bfloat16)
    image_back = jnp.einsum("arnf,fd->arnd", image_hid, image_down, preferred_element_type=jnp.float32)
    text_back = jnp.einsum("arnf,fd->arnd", text_hid, text_down, preferred_element_type=jnp.float32)
    mlp = scatter_slots(jnp.concatenate([image_back, text_back], 2).astype(jnp.bfloat16), "head")
    image_out = image_mid + per_request(image_mod[:, 5], image_mid, 0) * mlp[:, :image_tile]
    text_out = text_mid + per_request(text_mod[:, 5], text_mid, 0) * mlp[:, image_tile:]
    return image_out, text_out


def body(
    image_hidden,
    text_hidden,
    latent_grid,
    text_lengths,
    step_index,
    image_mod,
    text_mod,
    final_mod,
    image_qk_gain,
    text_qk_gain,
    image_qkv,
    text_qkv,
    image_proj,
    text_proj,
    image_up,
    text_up,
    image_down,
    text_down,
    final_proj,
    conv_kernel,
):
    blocks = lax.axis_size("blk")
    groups = lax.axis_size("head")
    requests, tile_rows, tile_cols, model_width = image_hidden.shape
    text_slice = text_hidden.shape[1]
    image_tile = tile_rows * tile_cols
    tile_tokens = image_tile + text_slice
    halves = []
    half = requests // 2
    for start in (0, half):
        pick = slice(start, start + half)
        halves.append(
            layer(image_hidden[pick], text_hidden[pick], text_lengths[pick], image_mod[pick],
                  text_mod[pick], image_qk_gain, text_qk_gain, image_qkv, text_qkv, image_proj,
                  text_proj, image_up, text_up, image_down, text_down)
        )
    image_out = jnp.concatenate([halves[0][0], halves[1][0]], 0)
    text_out = jnp.concatenate([halves[0][1], halves[1][1]], 0)
    image_states = image_out.reshape(requests, tile_rows, tile_cols, model_width).astype(jnp.bfloat16)
    text_states = text_out.astype(jnp.bfloat16)
    final_in = modulate(image_out, final_mod[:, 1], final_mod[:, 0], 0).astype(jnp.bfloat16)
    velocity = jnp.einsum("rnd,dp->rnp", final_in, final_proj, preferred_element_type=jnp.float32)
    channels = velocity.shape[-1] // 4
    velocity = (
        velocity.reshape(requests, tile_rows, tile_cols, 2, 2, channels)
        .transpose(0, 1, 3, 2, 4, 5)
        .reshape(requests, 2 * tile_rows, 2 * tile_cols, channels)
    )
    current = step_index.astype(jnp.float32) / 1000.0
    following = jnp.maximum(step_index - 125, 0).astype(jnp.float32) / 1000.0
    step_size = noise_level(following) - noise_level(current)
    latent_next = latent_grid + step_size[:, None, None, None] * velocity
    decoded_in = (latent_next / 1.5305 + 0.0609).astype(jnp.bfloat16)
    padded = extended(decoded_in, (("head", 1), ("blk", 2)), 1)
    features = convolve(padded, conv_kernel)
    return (image_states, text_states, latent_next, features)


def solution(mesh):
    in_specs = (
        P("req", "head", "blk", None),
        P("req", ("head", "blk"), None),
        P("req", "head", "blk", None),
        P("req"),
        P("req"),
        P("req", None, None),
        P("req", None, None),
        P("req", None, None),
        P(),
        P(),
        P(None, None, "head"),
        P(None, None, "head"),
        P("head", None),
        P("head", None),
        P(None, "head"),
        P(None, "head"),
        P("head", None),
        P("head", None),
        P(),
        P(),
    )
    out_specs = (
        P("req", "head", "blk", None),
        P("req", ("head", "blk"), None),
        P("req", "head", "blk", None),
        P("req", "head", "blk", None),
    )
    return jax.shard_map(body, mesh=mesh, in_specs=in_specs, out_specs=out_specs, check_vma=False)
```

```python
import math

import jax
import jax.numpy as jnp
from jax import lax
from jax.experimental import pallas as pl
from jax.sharding import PartitionSpec as P

HD = 64


def extended(block, sides, width):
    for axis, dim in sides:
        count = lax.axis_size(axis)
        forward = [(i, i + 1) for i in range(count - 1)]
        backward = [(target, source) for source, target in forward]
        low = lax.ppermute(
            lax.slice_in_dim(block, block.shape[dim] - width, None, axis=dim), axis, forward
        )
        high = lax.ppermute(lax.slice_in_dim(block, 0, width, axis=dim), axis, backward)
        block = jnp.concatenate([low, block, high], axis=dim)
    return block


def gather_slots(block, axis):
    count = lax.axis_size(axis)
    parts = [block]
    for shift in range(1, count):
        parts.append(lax.ppermute(block, axis, [(i, (i + shift) % count) for i in range(count)]))
    return jnp.stack(parts)


def scatter_slots(partial, axis):
    count = lax.axis_size(axis)
    total = partial[0].astype(jnp.float32)
    for shift in range(1, count):
        total = total + lax.ppermute(
            partial[shift], axis, [((i + shift) % count, i) for i in range(count)]
        ).astype(jnp.float32)
    return total


def send_slots(block, axis):
    count = lax.axis_size(axis)
    parts = [block]
    for shift in range(1, count):
        parts.append(lax.ppermute(block, axis, [(i, (i + shift) % count) for i in range(count)]))
    return parts


def attention_kernel(query_ref, *refs):
    *pair_refs, mask_ref, out_ref = refs
    query = query_ref[...]
    numerator = None
    denominator = None
    for block, pair_ref in enumerate(pair_refs):
        pairs = pair_ref[...]
        scores = lax.dot_general(
            query, pairs, (((1,), (1,)), ((), ())), preferred_element_type=jnp.float32
        ) * (1.0 / math.sqrt(HD))
        weights = jnp.exp(scores) * mask_ref[block]
        part_den = jnp.sum(weights, axis=1, keepdims=True)
        part_num = jnp.dot(weights.astype(jnp.bfloat16), pairs, preferred_element_type=jnp.float32)
        numerator = part_num if numerator is None else numerator + part_num
        denominator = part_den if denominator is None else denominator + part_den
    out_ref[...] = (numerator / denominator).astype(out_ref.dtype)


def attend(query_rows, pair_blocks, usable, heads, tile):
    requests, rows, lanes = query_rows.shape
    keys = pair_blocks[0].shape[0] // requests
    return pl.pallas_call(
        attention_kernel,
        grid=(requests, heads),
        in_specs=[pl.BlockSpec((None, rows, tile), lambda r, h: (r, 0, h))]
        + [pl.BlockSpec((keys, tile), lambda r, h: (r, h)) for _ in pair_blocks]
        + [pl.BlockSpec((None, len(pair_blocks), 1, keys), lambda r, h: (r, 0, 0, 0))],
        out_specs=pl.BlockSpec((None, rows, tile), lambda r, h: (r, 0, h)),
        out_shape=jax.ShapeDtypeStruct((requests, rows, lanes), jnp.bfloat16),
    )(query_rows, *pair_blocks, usable)


def per_request(vector, values, axis):
    shape = [1] * values.ndim
    shape[axis] = vector.shape[0]
    shape[-1] = vector.shape[-1]
    return vector.reshape(shape)


def modulate(values, shift, scale, axis):
    average = jnp.mean(values, -1, keepdims=True)
    centred = values - average
    spread = jnp.mean(centred * centred, -1, keepdims=True)
    normed = centred * lax.rsqrt(spread + 1e-06)
    return normed * (1.0 + per_request(scale, values, axis)) + per_request(shift, values, axis)


def head_norm(values, gain):
    width = values.shape[-1]
    lane_head = jnp.arange(width) // HD
    spread = (lane_head[:, None] == lane_head[None, :]).astype(jnp.float32) / HD
    mean_square = jnp.dot(values * values, spread, precision=lax.Precision.HIGHEST)
    return (values * lax.rsqrt(mean_square + 1e-06) * jnp.tile(gain, width // HD)).astype(jnp.bfloat16)


def noise_level(fraction):
    return 3.0 * fraction / (1.0 + 2.0 * fraction)


def attention_inputs(normed, weight, gains):
    model_width, _, local_width = weight.shape
    heads = local_width // HD
    split = weight.reshape(model_width, 3, heads, HD)
    query_weight = jnp.concatenate([split[:, 0], jnp.zeros_like(split[:, 0])], -1).reshape(
        model_width, 2 * local_width
    )
    pair_weight = jnp.concatenate([split[:, 1], split[:, 2]], -1).reshape(model_width, 2 * local_width)
    lane = jnp.arange(2 * local_width)
    live = (lane % (2 * HD)) < HD
    lane_head = lane // (2 * HD)
    spread = ((lane_head[:, None] == lane_head[None, :]) & live[:, None]).astype(jnp.float32) / HD
    query_gain = jnp.where(live, jnp.tile(jnp.concatenate([gains[0], gains[0]]), heads), 0.0)
    key_gain = jnp.tile(jnp.concatenate([gains[1], gains[1]]), heads)

    def normalized(values, gain):
        mean_square = jnp.dot(values * values, spread, precision=lax.Precision.HIGHEST)
        return values * lax.rsqrt(mean_square + 1e-06) * gain

    query_proj = jnp.einsum("arnd,de->arne", normed, query_weight, preferred_element_type=jnp.float32)
    pair_proj = jnp.einsum("arnd,de->arne", normed, pair_weight, preferred_element_type=jnp.float32)
    queries = normalized(query_proj, query_gain).astype(jnp.bfloat16)
    pairs = jnp.where(live, normalized(pair_proj, key_gain), pair_proj).astype(jnp.bfloat16)
    return queries, pairs


def convolve(padded, kernel):
    out_rows = padded.shape[1] - 2
    out_cols = padded.shape[2] - 2
    summed = jnp.zeros((padded.shape[0], out_rows, out_cols, kernel.shape[-1]), jnp.float32)
    for row_off in range(3):
        for col_off in range(3):
            summed = summed + jnp.einsum(
                "rhwc,co->rhwo",
                padded[:, row_off : row_off + out_rows, col_off : col_off + out_cols],
                kernel[row_off, col_off],
                preferred_element_type=jnp.float32,
            )
    return summed.astype(jnp.bfloat16)


def body(
    image_hidden,
    text_hidden,
    latent_grid,
    text_lengths,
    step_index,
    image_mod,
    text_mod,
    final_mod,
    image_qk_gain,
    text_qk_gain,
    image_qkv,
    text_qkv,
    image_proj,
    text_proj,
    image_up,
    text_up,
    image_down,
    text_down,
    final_proj,
    conv_kernel,
):
    blocks = lax.axis_size("blk")
    groups = lax.axis_size("head")
    requests, tile_rows, tile_cols, model_width = image_hidden.shape
    text_slice = text_hidden.shape[1]
    image_tile = tile_rows * tile_cols
    tile_tokens = image_tile + text_slice
    own = jnp.concatenate(
        [image_hidden.reshape(requests, image_tile, model_width), text_hidden], axis=1
    )
    strip = gather_slots(own, "head")
    strip_f = strip.astype(jnp.float32)
    image_x = strip_f[:, :, :image_tile]
    text_x = strip_f[:, :, image_tile:]
    image_norm = modulate(image_x, image_mod[:, 0], image_mod[:, 1], 1).astype(jnp.bfloat16)
    text_norm = modulate(text_x, text_mod[:, 0], text_mod[:, 1], 1).astype(jnp.bfloat16)
    image_q, image_kv = attention_inputs(image_norm, image_qkv, image_qk_gain)
    text_q, text_kv = attention_inputs(text_norm, text_qkv, text_qk_gain)
    queries = jnp.concatenate([image_q, text_q], 2)
    key_value = jnp.concatenate([image_kv, text_kv], 2)
    tile = 2 * HD
    local_heads = queries.shape[-1] // tile
    local_width = local_heads * HD
    score_scale = 1.0 / math.sqrt(HD)
    pair_blocks = send_slots(key_value.transpose(1, 0, 2, 3).reshape(-1, local_heads * tile), "blk")
    query_rows = groups * tile_tokens
    query_piece = queries.transpose(1, 0, 2, 3).reshape(requests, query_rows, local_heads * tile)
    position = jnp.arange(query_rows, dtype=jnp.int32)
    group = (lax.axis_index("head") - position // tile_tokens) % groups
    within = position % tile_tokens
    source = (lax.axis_index("blk") - jnp.arange(blocks, dtype=jnp.int32)) % blocks
    slot_ids = (group[None, :] * blocks + source[:, None]) * text_slice + (within - image_tile)[None, :]
    usable = (within < image_tile)[None, None, :] | (
        slot_ids[None, :, :] < text_lengths[:, None, None]
    )
    usable = usable.astype(jnp.float32).reshape(requests, blocks, 1, query_rows)
    attended = attend(query_piece, pair_blocks, usable, local_heads, tile)
    context = attended.reshape(requests, groups, tile_tokens, local_heads * tile)

    def padded_rows(weight):
        shaped = weight.reshape(local_heads, HD, weight.shape[-1])
        return jnp.concatenate([jnp.zeros_like(shaped), shaped], 1).reshape(local_heads * tile, -1)

    image_part = jnp.einsum(
        "rane,ed->arnd", context[:, :, :image_tile], padded_rows(image_proj), preferred_element_type=jnp.float32
    )
    text_part = jnp.einsum(
        "rane,ed->arnd", context[:, :, image_tile:], padded_rows(text_proj), preferred_element_type=jnp.float32
    )
    attn = scatter_slots(jnp.concatenate([image_part, text_part], 2).astype(jnp.bfloat16), "head")
    own_f = own.astype(jnp.float32)
    image_mid = own_f[:, :image_tile] + per_request(image_mod[:, 2], own_f, 0) * attn[:, :image_tile]
    text_mid = own_f[:, image_tile:] + per_request(text_mod[:, 2], own_f, 0) * attn[:, image_tile:]
    image_local = modulate(image_mid, image_mod[:, 3], image_mod[:, 4], 0).astype(jnp.bfloat16)
    text_local = modulate(text_mid, text_mod[:, 3], text_mod[:, 4], 0).astype(jnp.bfloat16)
    ff_in = gather_slots(jnp.concatenate([image_local, text_local], 1), "head")
    image_hid = jax.nn.gelu(
        jnp.einsum("arnd,df->arnf", ff_in[:, :, :image_tile], image_up, preferred_element_type=jnp.float32),
        approximate=True,
    ).astype(jnp.bfloat16)
    text_hid = jax.nn.gelu(
        jnp.einsum("arnd,df->arnf", ff_in[:, :, image_tile:], text_up, preferred_element_type=jnp.float32),
        approximate=True,
    ).astype(jnp.bfloat16)
    image_back = jnp.einsum("arnf,fd->arnd", image_hid, image_down, preferred_element_type=jnp.float32)
    text_back = jnp.einsum("arnf,fd->arnd", text_hid, text_down, preferred_element_type=jnp.float32)
    mlp = scatter_slots(jnp.concatenate([image_back, text_back], 2).astype(jnp.bfloat16), "head")
    image_out = image_mid + per_request(image_mod[:, 5], image_mid, 0) * mlp[:, :image_tile]
    text_out = text_mid + per_request(text_mod[:, 5], text_mid, 0) * mlp[:, image_tile:]
    image_states = image_out.reshape(requests, tile_rows, tile_cols, model_width).astype(jnp.bfloat16)
    text_states = text_out.astype(jnp.bfloat16)
    final_in = modulate(image_out, final_mod[:, 1], final_mod[:, 0], 0).astype(jnp.bfloat16)
    velocity = jnp.einsum("rnd,dp->rnp", final_in, final_proj, preferred_element_type=jnp.float32)
    channels = velocity.shape[-1] // 4
    velocity = (
        velocity.reshape(requests, tile_rows, tile_cols, 2, 2, channels)
        .transpose(0, 1, 3, 2, 4, 5)
        .reshape(requests, 2 * tile_rows, 2 * tile_cols, channels)
    )
    current = step_index.astype(jnp.float32) / 1000.0
    following = jnp.maximum(step_index - 125, 0).astype(jnp.float32) / 1000.0
    step_size = noise_level(following) - noise_level(current)
    latent_next = latent_grid + step_size[:, None, None, None] * velocity
    decoded_in = (latent_next / 1.5305 + 0.0609).astype(jnp.bfloat16)
    padded = extended(decoded_in, (("head", 1), ("blk", 2)), 1)
    features = convolve(padded, conv_kernel)
    return (image_states, text_states, latent_next, features)


def solution(mesh):
    in_specs = (
        P("req", "head", "blk", None),
        P("req", ("head", "blk"), None),
        P("req", "head", "blk", None),
        P("req"),
        P("req"),
        P("req", None, None),
        P("req", None, None),
        P("req", None, None),
        P(),
        P(),
        P(None, None, "head"),
        P(None, None, "head"),
        P("head", None),
        P("head", None),
        P(None, "head"),
        P(None, "head"),
        P("head", None),
        P("head", None),
        P(),
        P(),
    )
    out_specs = (
        P("req", "head", "blk", None),
        P("req", ("head", "blk"), None),
        P("req", "head", "blk", None),
        P("req", "head", "blk", None),
    )
    return jax.shard_map(body, mesh=mesh, in_specs=in_specs, out_specs=out_specs, check_vma=False)
```

```python
import math

import jax
import jax.numpy as jnp
from jax import lax
from jax.experimental import pallas as pl
from jax.sharding import PartitionSpec as P

HD = 64


def extended(block, sides, width):
    for axis, dim in sides:
        count = lax.axis_size(axis)
        forward = [(i, i + 1) for i in range(count - 1)]
        backward = [(target, source) for source, target in forward]
        low = lax.ppermute(
            lax.slice_in_dim(block, block.shape[dim] - width, None, axis=dim), axis, forward
        )
        high = lax.ppermute(lax.slice_in_dim(block, 0, width, axis=dim), axis, backward)
        block = jnp.concatenate([low, block, high], axis=dim)
    return block


def gather_slots(block, axis):
    count = lax.axis_size(axis)
    parts = [block]
    for shift in range(1, count):
        parts.append(lax.ppermute(block, axis, [(i, (i + shift) % count) for i in range(count)]))
    return jnp.stack(parts)


def scatter_slots(partial, axis):
    count = lax.axis_size(axis)
    total = partial[0].astype(jnp.float32)
    for shift in range(1, count):
        total = total + lax.ppermute(
            partial[shift], axis, [((i + shift) % count, i) for i in range(count)]
        ).astype(jnp.float32)
    return total


def send_slots(block, axis):
    count = lax.axis_size(axis)
    parts = [block]
    for shift in range(1, count):
        parts.append(lax.ppermute(block, axis, [(i, (i + shift) % count) for i in range(count)]))
    return parts


def attention_kernel(query_ref, *refs):
    *pair_refs, mask_ref, out_ref = refs
    query = query_ref[...]
    numerator = None
    denominator = None
    for block, pair_ref in enumerate(pair_refs):
        pairs = pair_ref[...]
        scores = lax.dot_general(
            query, pairs, (((1,), (1,)), ((), ())), preferred_element_type=jnp.float32
        ) * (1.0 / math.sqrt(HD))
        weights = jnp.exp(scores) * mask_ref[block]
        part_den = jnp.sum(weights, axis=1, keepdims=True)
        part_num = jnp.dot(weights.astype(jnp.bfloat16), pairs, preferred_element_type=jnp.float32)
        numerator = part_num if numerator is None else numerator + part_num
        denominator = part_den if denominator is None else denominator + part_den
    out_ref[...] = (numerator / denominator).astype(out_ref.dtype)


def attend(query_rows, pair_blocks, usable, heads, tile):
    requests, rows, lanes = query_rows.shape
    keys = pair_blocks[0].shape[0] // requests
    return pl.pallas_call(
        attention_kernel,
        grid=(requests, heads),
        in_specs=[pl.BlockSpec((None, rows, tile), lambda r, h: (r, 0, h))]
        + [pl.BlockSpec((keys, tile), lambda r, h: (r, h)) for _ in pair_blocks]
        + [pl.BlockSpec((None, len(pair_blocks), 1, keys), lambda r, h: (r, 0, 0, 0))],
        out_specs=pl.BlockSpec((None, rows, tile), lambda r, h: (r, 0, h)),
        out_shape=jax.ShapeDtypeStruct((requests, rows, lanes), jnp.bfloat16),
    )(query_rows, *pair_blocks, usable)


def return_slots(parts, axis):
    count = lax.axis_size(axis)
    total = parts[0].astype(jnp.float32)
    for shift in range(1, count):
        total = total + lax.ppermute(
            parts[shift], axis, [((i + shift) % count, i) for i in range(count)]
        ).astype(jnp.float32)
    return total


def per_request(vector, values, axis):
    shape = [1] * values.ndim
    shape[axis] = vector.shape[0]
    shape[-1] = vector.shape[-1]
    return vector.reshape(shape)


def modulate(values, shift, scale, axis):
    average = jnp.mean(values, -1, keepdims=True)
    centred = values - average
    spread = jnp.mean(centred * centred, -1, keepdims=True)
    normed = centred * lax.rsqrt(spread + 1e-06)
    return normed * (1.0 + per_request(scale, values, axis)) + per_request(shift, values, axis)


def head_norm(values, gain):
    width = values.shape[-1]
    lane_head = jnp.arange(width) // HD
    spread = (lane_head[:, None] == lane_head[None, :]).astype(jnp.float32) / HD
    mean_square = jnp.dot(values * values, spread, precision=lax.Precision.HIGHEST)
    return (values * lax.rsqrt(mean_square + 1e-06) * jnp.tile(gain, width // HD)).astype(jnp.bfloat16)


def noise_level(fraction):
    return 3.0 * fraction / (1.0 + 2.0 * fraction)


def attention_inputs(normed, weight, gains):
    model_width, _, local_width = weight.shape
    heads = local_width // HD
    split = weight.reshape(model_width, 3, heads, HD)
    query_weight = jnp.concatenate([split[:, 0], jnp.zeros_like(split[:, 0])], -1).reshape(
        model_width, 2 * local_width
    )
    pair_weight = jnp.concatenate([split[:, 1], split[:, 2]], -1).reshape(model_width, 2 * local_width)
    lane = jnp.arange(2 * local_width)
    live = (lane % (2 * HD)) < HD
    lane_head = lane // (2 * HD)
    spread = ((lane_head[:, None] == lane_head[None, :]) & live[:, None]).astype(jnp.float32) / HD
    query_gain = jnp.where(live, jnp.tile(jnp.concatenate([gains[0], gains[0]]), heads), 0.0)
    key_gain = jnp.tile(jnp.concatenate([gains[1], gains[1]]), heads)

    def normalized(values, gain):
        mean_square = jnp.dot(values * values, spread, precision=lax.Precision.HIGHEST)
        return values * lax.rsqrt(mean_square + 1e-06) * gain

    query_proj = jnp.einsum("arnd,de->arne", normed, query_weight, preferred_element_type=jnp.float32)
    pair_proj = jnp.einsum("arnd,de->arne", normed, pair_weight, preferred_element_type=jnp.float32)
    queries = normalized(query_proj, query_gain).astype(jnp.bfloat16)
    pairs = jnp.where(live, normalized(pair_proj, key_gain), pair_proj).astype(jnp.bfloat16)
    return queries, pairs


def convolve(padded, kernel):
    out_rows = padded.shape[1] - 2
    out_cols = padded.shape[2] - 2
    summed = jnp.zeros((padded.shape[0], out_rows, out_cols, kernel.shape[-1]), jnp.float32)
    for row_off in range(3):
        for col_off in range(3):
            summed = summed + jnp.einsum(
                "rhwc,co->rhwo",
                padded[:, row_off : row_off + out_rows, col_off : col_off + out_cols],
                kernel[row_off, col_off],
                preferred_element_type=jnp.float32,
            )
    return summed.astype(jnp.bfloat16)


def body(
    image_hidden,
    text_hidden,
    latent_grid,
    text_lengths,
    step_index,
    image_mod,
    text_mod,
    final_mod,
    image_qk_gain,
    text_qk_gain,
    image_qkv,
    text_qkv,
    image_proj,
    text_proj,
    image_up,
    text_up,
    image_down,
    text_down,
    final_proj,
    conv_kernel,
):
    blocks = lax.axis_size("blk")
    groups = lax.axis_size("head")
    requests, tile_rows, tile_cols, model_width = image_hidden.shape
    text_slice = text_hidden.shape[1]
    image_tile = tile_rows * tile_cols
    tile_tokens = image_tile + text_slice
    own = jnp.concatenate(
        [image_hidden.reshape(requests, image_tile, model_width), text_hidden], axis=1
    )
    strip = gather_slots(own, "head")
    strip_f = strip.astype(jnp.float32)
    image_x = strip_f[:, :, :image_tile]
    text_x = strip_f[:, :, image_tile:]
    image_norm = modulate(image_x, image_mod[:, 0], image_mod[:, 1], 1).astype(jnp.bfloat16)
    text_norm = modulate(text_x, text_mod[:, 0], text_mod[:, 1], 1).astype(jnp.bfloat16)
    image_q, image_kv = attention_inputs(image_norm, image_qkv, image_qk_gain)
    text_q, text_kv = attention_inputs(text_norm, text_qkv, text_qk_gain)
    queries = jnp.concatenate([image_q, text_q], 2)
    key_value = jnp.concatenate([image_kv, text_kv], 2)
    tile = 2 * HD
    local_heads = queries.shape[-1] // tile
    local_width = local_heads * HD
    score_scale = 1.0 / math.sqrt(HD)
    pair_blocks = send_slots(key_value.transpose(1, 0, 2, 3).reshape(-1, local_heads * tile), "blk")
    query_rows = groups * tile_tokens
    query_piece = queries.transpose(1, 0, 2, 3).reshape(requests, query_rows, local_heads * tile)
    position = jnp.arange(query_rows, dtype=jnp.int32)
    group = (lax.axis_index("head") - position // tile_tokens) % groups
    within = position % tile_tokens
    source = (lax.axis_index("blk") - jnp.arange(blocks, dtype=jnp.int32)) % blocks
    slot_ids = (group[None, :] * blocks + source[:, None]) * text_slice + (within - image_tile)[None, :]
    usable = (within < image_tile)[None, None, :] | (
        slot_ids[None, :, :] < text_lengths[:, None, None]
    )
    usable = usable.astype(jnp.float32).reshape(requests, blocks, 1, query_rows)
    attended = attend(query_piece, pair_blocks, usable, local_heads, tile)
    context = attended.reshape(requests, groups, tile_tokens, local_heads * tile)

    def padded_rows(weight):
        shaped = weight.reshape(local_heads, HD, weight.shape[-1])
        return jnp.concatenate([jnp.zeros_like(shaped), shaped], 1).reshape(local_heads * tile, -1)

    image_part = jnp.einsum(
        "rane,ed->arnd", context[:, :, :image_tile], padded_rows(image_proj), preferred_element_type=jnp.float32
    )
    text_part = jnp.einsum(
        "rane,ed->arnd", context[:, :, image_tile:], padded_rows(text_proj), preferred_element_type=jnp.float32
    )
    attn = scatter_slots(jnp.concatenate([image_part, text_part], 2).astype(jnp.bfloat16), "head")
    own_f = own.astype(jnp.float32)
    image_mid = own_f[:, :image_tile] + per_request(image_mod[:, 2], own_f, 0) * attn[:, :image_tile]
    text_mid = own_f[:, image_tile:] + per_request(text_mod[:, 2], own_f, 0) * attn[:, image_tile:]
    image_local = modulate(image_mid, image_mod[:, 3], image_mod[:, 4], 0).astype(jnp.bfloat16)
    text_local = modulate(text_mid, text_mod[:, 3], text_mod[:, 4], 0).astype(jnp.bfloat16)
    ff_blocks = send_slots(jnp.concatenate([image_local, text_local], 1), "head")
    ff_parts = []
    half = groups // 2
    for first in (0, half):
        ff_in = jnp.stack(ff_blocks[first:first + half])
        image_hid = jax.nn.gelu(
            jnp.einsum("arnd,df->arnf", ff_in[:, :, :image_tile], image_up, preferred_element_type=jnp.float32),
            approximate=True,
        ).astype(jnp.bfloat16)
        text_hid = jax.nn.gelu(
            jnp.einsum("arnd,df->arnf", ff_in[:, :, image_tile:], text_up, preferred_element_type=jnp.float32),
            approximate=True,
        ).astype(jnp.bfloat16)
        image_back = jnp.einsum("arnf,fd->arnd", image_hid, image_down, preferred_element_type=jnp.float32)
        text_back = jnp.einsum("arnf,fd->arnd", text_hid, text_down, preferred_element_type=jnp.float32)
        back = jnp.concatenate([image_back, text_back], 2).astype(jnp.bfloat16)
        ff_parts.extend(back[k] for k in range(half))
    mlp = return_slots(ff_parts, "head")
    image_out = image_mid + per_request(image_mod[:, 5], image_mid, 0) * mlp[:, :image_tile]
    text_out = text_mid + per_request(text_mod[:, 5], text_mid, 0) * mlp[:, image_tile:]
    image_states = image_out.reshape(requests, tile_rows, tile_cols, model_width).astype(jnp.bfloat16)
    text_states = text_out.astype(jnp.bfloat16)
    final_in = modulate(image_out, final_mod[:, 1], final_mod[:, 0], 0).astype(jnp.bfloat16)
    velocity = jnp.einsum("rnd,dp->rnp", final_in, final_proj, preferred_element_type=jnp.float32)
    channels = velocity.shape[-1] // 4
    velocity = (
        velocity.reshape(requests, tile_rows, tile_cols, 2, 2, channels)
        .transpose(0, 1, 3, 2, 4, 5)
        .reshape(requests, 2 * tile_rows, 2 * tile_cols, channels)
    )
    current = step_index.astype(jnp.float32) / 1000.0
    following = jnp.maximum(step_index - 125, 0).astype(jnp.float32) / 1000.0
    step_size = noise_level(following) - noise_level(current)
    latent_next = latent_grid + step_size[:, None, None, None] * velocity
    decoded_in = (latent_next / 1.5305 + 0.0609).astype(jnp.bfloat16)
    padded = extended(decoded_in, (("head", 1), ("blk", 2)), 1)
    features = convolve(padded, conv_kernel)
    return (image_states, text_states, latent_next, features)


def solution(mesh):
    in_specs = (
        P("req", "head", "blk", None),
        P("req", ("head", "blk"), None),
        P("req", "head", "blk", None),
        P("req"),
        P("req"),
        P("req", None, None),
        P("req", None, None),
        P("req", None, None),
        P(),
        P(),
        P(None, None, "head"),
        P(None, None, "head"),
        P("head", None),
        P("head", None),
        P(None, "head"),
        P(None, "head"),
        P("head", None),
        P("head", None),
        P(),
        P(),
    )
    out_specs = (
        P("req", "head", "blk", None),
        P("req", ("head", "blk"), None),
        P("req", "head", "blk", None),
        P("req", "head", "blk", None),
    )
    return jax.shard_map(body, mesh=mesh, in_specs=in_specs, out_specs=out_specs, check_vma=False)
```

```python
import math

import jax
import jax.numpy as jnp
from jax import lax
from jax.experimental import pallas as pl
from jax.sharding import PartitionSpec as P

HD = 64


def extended(block, sides, width):
    for axis, dim in sides:
        count = lax.axis_size(axis)
        forward = [(i, i + 1) for i in range(count - 1)]
        backward = [(target, source) for source, target in forward]
        low = lax.ppermute(
            lax.slice_in_dim(block, block.shape[dim] - width, None, axis=dim), axis, forward
        )
        high = lax.ppermute(lax.slice_in_dim(block, 0, width, axis=dim), axis, backward)
        block = jnp.concatenate([low, block, high], axis=dim)
    return block


def gather_slots(block, axis):
    count = lax.axis_size(axis)
    parts = [block]
    for shift in range(1, count):
        parts.append(lax.ppermute(block, axis, [(i, (i + shift) % count) for i in range(count)]))
    return jnp.stack(parts)


def scatter_slots(partial, axis):
    count = lax.axis_size(axis)
    total = partial[0].astype(jnp.float32)
    for shift in range(1, count):
        total = total + lax.ppermute(
            partial[shift], axis, [((i + shift) % count, i) for i in range(count)]
        ).astype(jnp.float32)
    return total


def send_slots(block, axis):
    count = lax.axis_size(axis)
    parts = [block]
    for shift in range(1, count):
        parts.append(lax.ppermute(block, axis, [(i, (i + shift) % count) for i in range(count)]))
    return parts


def attention_kernel(query_ref, *refs):
    *pair_refs, mask_ref, out_ref = refs
    query = query_ref[...]
    numerator = None
    denominator = None
    for block, pair_ref in enumerate(pair_refs):
        pairs = pair_ref[...]
        scores = lax.dot_general(
            query, pairs, (((1,), (1,)), ((), ())), preferred_element_type=jnp.float32
        ) * (1.0 / math.sqrt(HD))
        weights = jnp.exp(scores) * mask_ref[block]
        part_den = jnp.sum(weights, axis=1, keepdims=True)
        part_num = jnp.dot(weights.astype(jnp.bfloat16), pairs, preferred_element_type=jnp.float32)
        numerator = part_num if numerator is None else numerator + part_num
        denominator = part_den if denominator is None else denominator + part_den
    out_ref[...] = (numerator / denominator).astype(out_ref.dtype)


def attend(query_rows, pair_blocks, usable, heads, tile):
    requests, rows, lanes = query_rows.shape
    keys = pair_blocks[0].shape[0] // requests
    return pl.pallas_call(
        attention_kernel,
        grid=(requests, heads),
        in_specs=[pl.BlockSpec((None, rows, tile), lambda r, h: (r, 0, h))]
        + [pl.BlockSpec((keys, tile), lambda r, h: (r, h)) for _ in pair_blocks]
        + [pl.BlockSpec((None, len(pair_blocks), 1, keys), lambda r, h: (r, 0, 0, 0))],
        out_specs=pl.BlockSpec((None, rows, tile), lambda r, h: (r, 0, h)),
        out_shape=jax.ShapeDtypeStruct((requests, rows, lanes), jnp.bfloat16),
    )(query_rows, *pair_blocks, usable)


def per_request(vector, values, axis):
    shape = [1] * values.ndim
    shape[axis] = vector.shape[0]
    shape[-1] = vector.shape[-1]
    return vector.reshape(shape)


def modulate(values, shift, scale, axis):
    average = jnp.mean(values, -1, keepdims=True)
    centred = values - average
    spread = jnp.mean(centred * centred, -1, keepdims=True)
    normed = centred * lax.rsqrt(spread + 1e-06)
    return normed * (1.0 + per_request(scale, values, axis)) + per_request(shift, values, axis)


def head_norm(values, gain):
    width = values.shape[-1]
    lane_head = jnp.arange(width) // HD
    spread = (lane_head[:, None] == lane_head[None, :]).astype(jnp.float32) / HD
    mean_square = jnp.dot(values * values, spread, precision=lax.Precision.HIGHEST)
    return (values * lax.rsqrt(mean_square + 1e-06) * jnp.tile(gain, width // HD)).astype(jnp.bfloat16)


def noise_level(fraction):
    return 3.0 * fraction / (1.0 + 2.0 * fraction)


def attention_inputs(normed, weight, gains):
    model_width, _, local_width = weight.shape
    heads = local_width // HD
    split = weight.reshape(model_width, 3, heads, HD)
    query_weight = jnp.concatenate([split[:, 0], jnp.zeros_like(split[:, 0])], -1).reshape(
        model_width, 2 * local_width
    )
    pair_weight = jnp.concatenate([split[:, 1], split[:, 2]], -1).reshape(model_width, 2 * local_width)
    lane = jnp.arange(2 * local_width)
    live = (lane % (2 * HD)) < HD
    lane_head = lane // (2 * HD)
    spread = ((lane_head[:, None] == lane_head[None, :]) & live[:, None]).astype(jnp.float32) / HD
    query_gain = jnp.where(live, jnp.tile(jnp.concatenate([gains[0], gains[0]]), heads), 0.0)
    key_gain = jnp.tile(jnp.concatenate([gains[1], gains[1]]), heads)

    def normalized(values, gain):
        mean_square = jnp.dot(values * values, spread, precision=lax.Precision.HIGHEST)
        return values * lax.rsqrt(mean_square + 1e-06) * gain

    query_proj = jnp.einsum("arnd,de->arne", normed, query_weight, preferred_element_type=jnp.float32)
    pair_proj = jnp.einsum("arnd,de->arne", normed, pair_weight, preferred_element_type=jnp.float32)
    queries = normalized(query_proj, query_gain).astype(jnp.bfloat16)
    pairs = jnp.where(live, normalized(pair_proj, key_gain), pair_proj).astype(jnp.bfloat16)
    return queries, pairs


def convolve(padded, kernel):
    out_rows = padded.shape[1] - 2
    out_cols = padded.shape[2] - 2
    summed = jnp.zeros((padded.shape[0], out_rows, out_cols, kernel.shape[-1]), jnp.float32)
    for row_off in range(3):
        for col_off in range(3):
            summed = summed + jnp.einsum(
                "rhwc,co->rhwo",
                padded[:, row_off : row_off + out_rows, col_off : col_off + out_cols],
                kernel[row_off, col_off],
                preferred_element_type=jnp.float32,
            )
    return summed.astype(jnp.bfloat16)


def body(
    image_hidden,
    text_hidden,
    latent_grid,
    text_lengths,
    step_index,
    image_mod,
    text_mod,
    final_mod,
    image_qk_gain,
    text_qk_gain,
    image_qkv,
    text_qkv,
    image_proj,
    text_proj,
    image_up,
    text_up,
    image_down,
    text_down,
    final_proj,
    conv_kernel,
):
    blocks = lax.axis_size("blk")
    groups = lax.axis_size("head")
    requests, tile_rows, tile_cols, model_width = image_hidden.shape
    text_slice = text_hidden.shape[1]
    image_tile = tile_rows * tile_cols
    tile_tokens = image_tile + text_slice
    own = jnp.concatenate(
        [image_hidden.reshape(requests, image_tile, model_width), text_hidden], axis=1
    )
    strip = gather_slots(own, "head")
    strip_f = strip.astype(jnp.float32)
    image_x = strip_f[:, :, :image_tile]
    text_x = strip_f[:, :, image_tile:]
    image_norm = modulate(image_x, image_mod[:, 0], image_mod[:, 1], 1).astype(jnp.bfloat16)
    text_norm = modulate(text_x, text_mod[:, 0], text_mod[:, 1], 1).astype(jnp.bfloat16)
    image_q, image_kv = attention_inputs(image_norm, image_qkv, image_qk_gain)
    text_q, text_kv = attention_inputs(text_norm, text_qkv, text_qk_gain)
    queries = jnp.concatenate([image_q, text_q], 2)
    key_value = jnp.concatenate([image_kv, text_kv], 2)
    tile = 2 * HD
    local_heads = queries.shape[-1] // tile
    local_width = local_heads * HD
    score_scale = 1.0 / math.sqrt(HD)
    own_pairs = key_value.transpose(1, 0, 2, 3).reshape(-1, local_heads * tile)
    flip_core = [(j, j ^ 1) for j in range(blocks)]
    flip_chip = [(j, j ^ 2) for j in range(blocks)]
    far = lax.ppermute(own_pairs, "blk", flip_chip)
    pair_blocks = [
        own_pairs,
        lax.ppermute(own_pairs, "blk", flip_core),
        far,
        lax.ppermute(far, "blk", flip_core),
    ]
    query_rows = groups * tile_tokens
    query_piece = queries.transpose(1, 0, 2, 3).reshape(requests, query_rows, local_heads * tile)
    position = jnp.arange(query_rows, dtype=jnp.int32)
    group = (lax.axis_index("head") - position // tile_tokens) % groups
    within = position % tile_tokens
    source = jnp.bitwise_xor(lax.axis_index("blk"), jnp.arange(blocks, dtype=jnp.int32))
    slot_ids = (group[None, :] * blocks + source[:, None]) * text_slice + (within - image_tile)[None, :]
    usable = (within < image_tile)[None, None, :] | (
        slot_ids[None, :, :] < text_lengths[:, None, None]
    )
    usable = usable.astype(jnp.float32).reshape(requests, blocks, 1, query_rows)
    attended = attend(query_piece, pair_blocks, usable, local_heads, tile)
    context = attended.reshape(requests, groups, tile_tokens, local_heads * tile)

    def padded_rows(weight):
        shaped = weight.reshape(local_heads, HD, weight.shape[-1])
        return jnp.concatenate([jnp.zeros_like(shaped), shaped], 1).reshape(local_heads * tile, -1)

    image_part = jnp.einsum(
        "rane,ed->arnd", context[:, :, :image_tile], padded_rows(image_proj), preferred_element_type=jnp.float32
    )
    text_part = jnp.einsum(
        "rane,ed->arnd", context[:, :, image_tile:], padded_rows(text_proj), preferred_element_type=jnp.float32
    )
    attn = scatter_slots(jnp.concatenate([image_part, text_part], 2).astype(jnp.bfloat16), "head")
    own_f = own.astype(jnp.float32)
    image_mid = own_f[:, :image_tile] + per_request(image_mod[:, 2], own_f, 0) * attn[:, :image_tile]
    text_mid = own_f[:, image_tile:] + per_request(text_mod[:, 2], own_f, 0) * attn[:, image_tile:]
    image_local = modulate(image_mid, image_mod[:, 3], image_mod[:, 4], 0).astype(jnp.bfloat16)
    text_local = modulate(text_mid, text_mod[:, 3], text_mod[:, 4], 0).astype(jnp.bfloat16)
    ff_in = gather_slots(jnp.concatenate([image_local, text_local], 1), "head")
    image_hid = jax.nn.gelu(
        jnp.einsum("arnd,df->arnf", ff_in[:, :, :image_tile], image_up, preferred_element_type=jnp.float32),
        approximate=True,
    ).astype(jnp.bfloat16)
    text_hid = jax.nn.gelu(
        jnp.einsum("arnd,df->arnf", ff_in[:, :, image_tile:], text_up, preferred_element_type=jnp.float32),
        approximate=True,
    ).astype(jnp.bfloat16)
    image_back = jnp.einsum("arnf,fd->arnd", image_hid, image_down, preferred_element_type=jnp.float32)
    text_back = jnp.einsum("arnf,fd->arnd", text_hid, text_down, preferred_element_type=jnp.float32)
    mlp = scatter_slots(jnp.concatenate([image_back, text_back], 2).astype(jnp.bfloat16), "head")
    image_out = image_mid + per_request(image_mod[:, 5], image_mid, 0) * mlp[:, :image_tile]
    text_out = text_mid + per_request(text_mod[:, 5], text_mid, 0) * mlp[:, image_tile:]
    image_states = image_out.reshape(requests, tile_rows, tile_cols, model_width).astype(jnp.bfloat16)
    text_states = text_out.astype(jnp.bfloat16)
    final_in = modulate(image_out, final_mod[:, 1], final_mod[:, 0], 0).astype(jnp.bfloat16)
    velocity = jnp.einsum("rnd,dp->rnp", final_in, final_proj, preferred_element_type=jnp.float32)
    channels = velocity.shape[-1] // 4
    velocity = (
        velocity.reshape(requests, tile_rows, tile_cols, 2, 2, channels)
        .transpose(0, 1, 3, 2, 4, 5)
        .reshape(requests, 2 * tile_rows, 2 * tile_cols, channels)
    )
    current = step_index.astype(jnp.float32) / 1000.0
    following = jnp.maximum(step_index - 125, 0).astype(jnp.float32) / 1000.0
    step_size = noise_level(following) - noise_level(current)
    latent_next = latent_grid + step_size[:, None, None, None] * velocity
    decoded_in = (latent_next / 1.5305 + 0.0609).astype(jnp.bfloat16)
    padded = extended(decoded_in, (("head", 1), ("blk", 2)), 1)
    features = convolve(padded, conv_kernel)
    return (image_states, text_states, latent_next, features)


def solution(mesh):
    in_specs = (
        P("req", "head", "blk", None),
        P("req", ("head", "blk"), None),
        P("req", "head", "blk", None),
        P("req"),
        P("req"),
        P("req", None, None),
        P("req", None, None),
        P("req", None, None),
        P(),
        P(),
        P(None, None, "head"),
        P(None, None, "head"),
        P("head", None),
        P("head", None),
        P(None, "head"),
        P(None, "head"),
        P("head", None),
        P("head", None),
        P(),
        P(),
    )
    out_specs = (
        P("req", "head", "blk", None),
        P("req", ("head", "blk"), None),
        P("req", "head", "blk", None),
        P("req", "head", "blk", None),
    )
    return jax.shard_map(body, mesh=mesh, in_specs=in_specs, out_specs=out_specs, check_vma=False)
```

```python
import math

import jax
import jax.numpy as jnp
from jax import lax
from jax.experimental import pallas as pl
from jax.sharding import PartitionSpec as P

HD = 64


def extended(block, sides, width):
    for axis, dim in sides:
        count = lax.axis_size(axis)
        forward = [(i, i + 1) for i in range(count - 1)]
        backward = [(target, source) for source, target in forward]
        low = lax.ppermute(
            lax.slice_in_dim(block, block.shape[dim] - width, None, axis=dim), axis, forward
        )
        high = lax.ppermute(lax.slice_in_dim(block, 0, width, axis=dim), axis, backward)
        block = jnp.concatenate([low, block, high], axis=dim)
    return block


def gather_slots(block, axis):
    count = lax.axis_size(axis)
    parts = [block]
    for shift in range(1, count):
        parts.append(lax.ppermute(block, axis, [(i, (i + shift) % count) for i in range(count)]))
    return jnp.stack(parts)


def scatter_slots(partial, axis):
    count = lax.axis_size(axis)
    total = partial[0].astype(jnp.float32)
    for shift in range(1, count):
        total = total + lax.ppermute(
            partial[shift], axis, [((i + shift) % count, i) for i in range(count)]
        ).astype(jnp.float32)
    return total


def send_slots(block, axis):
    count = lax.axis_size(axis)
    parts = [block]
    for shift in range(1, count):
        parts.append(lax.ppermute(block, axis, [(i, (i + shift) % count) for i in range(count)]))
    return parts


def attention_sums(query, pair_refs, mask_ref, first):
    numerator = None
    denominator = None
    for block, pair_ref in enumerate(pair_refs):
        pairs = pair_ref[...]
        scores = lax.dot_general(
            query, pairs, (((1,), (1,)), ((), ())), preferred_element_type=jnp.float32
        ) * (1.0 / math.sqrt(HD))
        weights = jnp.exp(scores) * mask_ref[first + block]
        part_den = jnp.sum(weights, axis=1, keepdims=True)
        part_num = jnp.dot(weights.astype(jnp.bfloat16), pairs, preferred_element_type=jnp.float32)
        numerator = part_num if numerator is None else numerator + part_num
        denominator = part_den if denominator is None else denominator + part_den
    return numerator, denominator


def near_kernel(query_ref, *refs):
    *pair_refs, mask_ref, num_ref, den_ref = refs
    numerator, denominator = attention_sums(query_ref[...], pair_refs, mask_ref, 0)
    num_ref[...] = numerator
    den_ref[...] = denominator


def far_kernel(query_ref, *refs):
    *pair_refs, mask_ref, num_in_ref, den_in_ref, out_ref = refs
    numerator, denominator = attention_sums(query_ref[...], pair_refs, mask_ref, len(pair_refs))
    out_ref[...] = ((numerator + num_in_ref[...]) / (denominator + den_in_ref[...])).astype(out_ref.dtype)


def attend(query_rows, pair_blocks, usable, heads, tile):
    requests, rows, lanes = query_rows.shape
    keys = pair_blocks[0].shape[0] // requests
    half = len(pair_blocks) // 2
    row_spec = pl.BlockSpec((None, rows, tile), lambda r, h: (r, 0, h))
    pair_spec = pl.BlockSpec((keys, tile), lambda r, h: (r, h))
    mask_spec = pl.BlockSpec((None, len(pair_blocks), 1, keys), lambda r, h: (r, 0, 0, 0))
    den_spec = pl.BlockSpec((None, None, rows, 1), lambda r, h: (r, h, 0, 0))
    numerator, denominator = pl.pallas_call(
        near_kernel,
        grid=(requests, heads),
        in_specs=[row_spec] + [pair_spec] * half + [mask_spec],
        out_specs=[row_spec, den_spec],
        out_shape=[
            jax.ShapeDtypeStruct((requests, rows, lanes), jnp.float32),
            jax.ShapeDtypeStruct((requests, heads, rows, 1), jnp.float32),
        ],
    )(query_rows, *pair_blocks[:half], usable)
    return pl.pallas_call(
        far_kernel,
        grid=(requests, heads),
        in_specs=[row_spec] + [pair_spec] * half + [mask_spec, row_spec, den_spec],
        out_specs=row_spec,
        out_shape=jax.ShapeDtypeStruct((requests, rows, lanes), jnp.bfloat16),
    )(query_rows, *pair_blocks[half:], usable, numerator, denominator)


def per_request(vector, values, axis):
    shape = [1] * values.ndim
    shape[axis] = vector.shape[0]
    shape[-1] = vector.shape[-1]
    return vector.reshape(shape)


def modulate(values, shift, scale, axis):
    average = jnp.mean(values, -1, keepdims=True)
    centred = values - average
    spread = jnp.mean(centred * centred, -1, keepdims=True)
    normed = centred * lax.rsqrt(spread + 1e-06)
    return normed * (1.0 + per_request(scale, values, axis)) + per_request(shift, values, axis)


def head_norm(values, gain):
    width = values.shape[-1]
    lane_head = jnp.arange(width) // HD
    spread = (lane_head[:, None] == lane_head[None, :]).astype(jnp.float32) / HD
    mean_square = jnp.dot(values * values, spread, precision=lax.Precision.HIGHEST)
    return (values * lax.rsqrt(mean_square + 1e-06) * jnp.tile(gain, width // HD)).astype(jnp.bfloat16)


def noise_level(fraction):
    return 3.0 * fraction / (1.0 + 2.0 * fraction)


def attention_inputs(normed, weight, gains):
    model_width, _, local_width = weight.shape
    heads = local_width // HD
    split = weight.reshape(model_width, 3, heads, HD)
    query_weight = jnp.concatenate([split[:, 0], jnp.zeros_like(split[:, 0])], -1).reshape(
        model_width, 2 * local_width
    )
    pair_weight = jnp.concatenate([split[:, 1], split[:, 2]], -1).reshape(model_width, 2 * local_width)
    lane = jnp.arange(2 * local_width)
    live = (lane % (2 * HD)) < HD
    lane_head = lane // (2 * HD)
    spread = ((lane_head[:, None] == lane_head[None, :]) & live[:, None]).astype(jnp.float32) / HD
    query_gain = jnp.where(live, jnp.tile(jnp.concatenate([gains[0], gains[0]]), heads), 0.0)
    key_gain = jnp.tile(jnp.concatenate([gains[1], gains[1]]), heads)

    def normalized(values, gain):
        mean_square = jnp.dot(values * values, spread, precision=lax.Precision.HIGHEST)
        return values * lax.rsqrt(mean_square + 1e-06) * gain

    query_proj = jnp.einsum("arnd,de->arne", normed, query_weight, preferred_element_type=jnp.float32)
    pair_proj = jnp.einsum("arnd,de->arne", normed, pair_weight, preferred_element_type=jnp.float32)
    queries = normalized(query_proj, query_gain).astype(jnp.bfloat16)
    pairs = jnp.where(live, normalized(pair_proj, key_gain), pair_proj).astype(jnp.bfloat16)
    return queries, pairs


def convolve(padded, kernel):
    out_rows = padded.shape[1] - 2
    out_cols = padded.shape[2] - 2
    summed = jnp.zeros((padded.shape[0], out_rows, out_cols, kernel.shape[-1]), jnp.float32)
    for row_off in range(3):
        for col_off in range(3):
            summed = summed + jnp.einsum(
                "rhwc,co->rhwo",
                padded[:, row_off : row_off + out_rows, col_off : col_off + out_cols],
                kernel[row_off, col_off],
                preferred_element_type=jnp.float32,
            )
    return summed.astype(jnp.bfloat16)


def body(
    image_hidden,
    text_hidden,
    latent_grid,
    text_lengths,
    step_index,
    image_mod,
    text_mod,
    final_mod,
    image_qk_gain,
    text_qk_gain,
    image_qkv,
    text_qkv,
    image_proj,
    text_proj,
    image_up,
    text_up,
    image_down,
    text_down,
    final_proj,
    conv_kernel,
):
    blocks = lax.axis_size("blk")
    groups = lax.axis_size("head")
    requests, tile_rows, tile_cols, model_width = image_hidden.shape
    text_slice = text_hidden.shape[1]
    image_tile = tile_rows * tile_cols
    tile_tokens = image_tile + text_slice
    own = jnp.concatenate(
        [image_hidden.reshape(requests, image_tile, model_width), text_hidden], axis=1
    )
    strip = gather_slots(own, "head")
    strip_f = strip.astype(jnp.float32)
    image_x = strip_f[:, :, :image_tile]
    text_x = strip_f[:, :, image_tile:]
    image_norm = modulate(image_x, image_mod[:, 0], image_mod[:, 1], 1).astype(jnp.bfloat16)
    text_norm = modulate(text_x, text_mod[:, 0], text_mod[:, 1], 1).astype(jnp.bfloat16)
    image_q, image_kv = attention_inputs(image_norm, image_qkv, image_qk_gain)
    text_q, text_kv = attention_inputs(text_norm, text_qkv, text_qk_gain)
    queries = jnp.concatenate([image_q, text_q], 2)
    key_value = jnp.concatenate([image_kv, text_kv], 2)
    tile = 2 * HD
    local_heads = queries.shape[-1] // tile
    local_width = local_heads * HD
    score_scale = 1.0 / math.sqrt(HD)
    own_pairs = key_value.transpose(1, 0, 2, 3).reshape(-1, local_heads * tile)
    flip_core = [(j, j ^ 1) for j in range(blocks)]
    flip_chip = [(j, j ^ 2) for j in range(blocks)]
    far = lax.ppermute(own_pairs, "blk", flip_chip)
    pair_blocks = [
        own_pairs,
        lax.ppermute(own_pairs, "blk", flip_core),
        far,
        lax.ppermute(far, "blk", flip_core),
    ]
    query_rows = groups * tile_tokens
    query_piece = queries.transpose(1, 0, 2, 3).reshape(requests, query_rows, local_heads * tile)
    position = jnp.arange(query_rows, dtype=jnp.int32)
    group = (lax.axis_index("head") - position // tile_tokens) % groups
    within = position % tile_tokens
    source = jnp.bitwise_xor(lax.axis_index("blk"), jnp.arange(blocks, dtype=jnp.int32))
    slot_ids = (group[None, :] * blocks + source[:, None]) * text_slice + (within - image_tile)[None, :]
    usable = (within < image_tile)[None, None, :] | (
        slot_ids[None, :, :] < text_lengths[:, None, None]
    )
    usable = usable.astype(jnp.float32).reshape(requests, blocks, 1, query_rows)
    attended = attend(query_piece, pair_blocks, usable, local_heads, tile)
    context = attended.reshape(requests, groups, tile_tokens, local_heads * tile)

    def padded_rows(weight):
        shaped = weight.reshape(local_heads, HD, weight.shape[-1])
        return jnp.concatenate([jnp.zeros_like(shaped), shaped], 1).reshape(local_heads * tile, -1)

    image_part = jnp.einsum(
        "rane,ed->arnd", context[:, :, :image_tile], padded_rows(image_proj), preferred_element_type=jnp.float32
    )
    text_part = jnp.einsum(
        "rane,ed->arnd", context[:, :, image_tile:], padded_rows(text_proj), preferred_element_type=jnp.float32
    )
    attn = scatter_slots(jnp.concatenate([image_part, text_part], 2).astype(jnp.bfloat16), "head")
    own_f = own.astype(jnp.float32)
    image_mid = own_f[:, :image_tile] + per_request(image_mod[:, 2], own_f, 0) * attn[:, :image_tile]
    text_mid = own_f[:, image_tile:] + per_request(text_mod[:, 2], own_f, 0) * attn[:, image_tile:]
    image_local = modulate(image_mid, image_mod[:, 3], image_mod[:, 4], 0).astype(jnp.bfloat16)
    text_local = modulate(text_mid, text_mod[:, 3], text_mod[:, 4], 0).astype(jnp.bfloat16)
    ff_in = gather_slots(jnp.concatenate([image_local, text_local], 1), "head")
    image_hid = jax.nn.gelu(
        jnp.einsum("arnd,df->arnf", ff_in[:, :, :image_tile], image_up, preferred_element_type=jnp.float32),
        approximate=True,
    ).astype(jnp.bfloat16)
    text_hid = jax.nn.gelu(
        jnp.einsum("arnd,df->arnf", ff_in[:, :, image_tile:], text_up, preferred_element_type=jnp.float32),
        approximate=True,
    ).astype(jnp.bfloat16)
    image_back = jnp.einsum("arnf,fd->arnd", image_hid, image_down, preferred_element_type=jnp.float32)
    text_back = jnp.einsum("arnf,fd->arnd", text_hid, text_down, preferred_element_type=jnp.float32)
    mlp = scatter_slots(jnp.concatenate([image_back, text_back], 2).astype(jnp.bfloat16), "head")
    image_out = image_mid + per_request(image_mod[:, 5], image_mid, 0) * mlp[:, :image_tile]
    text_out = text_mid + per_request(text_mod[:, 5], text_mid, 0) * mlp[:, image_tile:]
    image_states = image_out.reshape(requests, tile_rows, tile_cols, model_width).astype(jnp.bfloat16)
    text_states = text_out.astype(jnp.bfloat16)
    final_in = modulate(image_out, final_mod[:, 1], final_mod[:, 0], 0).astype(jnp.bfloat16)
    velocity = jnp.einsum("rnd,dp->rnp", final_in, final_proj, preferred_element_type=jnp.float32)
    channels = velocity.shape[-1] // 4
    velocity = (
        velocity.reshape(requests, tile_rows, tile_cols, 2, 2, channels)
        .transpose(0, 1, 3, 2, 4, 5)
        .reshape(requests, 2 * tile_rows, 2 * tile_cols, channels)
    )
    current = step_index.astype(jnp.float32) / 1000.0
    following = jnp.maximum(step_index - 125, 0).astype(jnp.float32) / 1000.0
    step_size = noise_level(following) - noise_level(current)
    latent_next = latent_grid + step_size[:, None, None, None] * velocity
    decoded_in = (latent_next / 1.5305 + 0.0609).astype(jnp.bfloat16)
    padded = extended(decoded_in, (("head", 1), ("blk", 2)), 1)
    features = convolve(padded, conv_kernel)
    return (image_states, text_states, latent_next, features)


def solution(mesh):
    in_specs = (
        P("req", "head", "blk", None),
        P("req", ("head", "blk"), None),
        P("req", "head", "blk", None),
        P("req"),
        P("req"),
        P("req", None, None),
        P("req", None, None),
        P("req", None, None),
        P(),
        P(),
        P(None, None, "head"),
        P(None, None, "head"),
        P("head", None),
        P("head", None),
        P(None, "head"),
        P(None, "head"),
        P("head", None),
        P("head", None),
        P(),
        P(),
    )
    out_specs = (
        P("req", "head", "blk", None),
        P("req", ("head", "blk"), None),
        P("req", "head", "blk", None),
        P("req", "head", "blk", None),
    )
    return jax.shard_map(body, mesh=mesh, in_specs=in_specs, out_specs=out_specs, check_vma=False)
```

```python
import math

import jax
import jax.numpy as jnp
from jax import lax
from jax.experimental import pallas as pl
from jax.sharding import PartitionSpec as P

HD = 64


def extended(block, sides, width):
    for axis, dim in sides:
        count = lax.axis_size(axis)
        forward = [(i, i + 1) for i in range(count - 1)]
        backward = [(target, source) for source, target in forward]
        low = lax.ppermute(
            lax.slice_in_dim(block, block.shape[dim] - width, None, axis=dim), axis, forward
        )
        high = lax.ppermute(lax.slice_in_dim(block, 0, width, axis=dim), axis, backward)
        block = jnp.concatenate([low, block, high], axis=dim)
    return block


def gather_slots(block, axis):
    count = lax.axis_size(axis)
    parts = [block]
    for shift in range(1, count):
        parts.append(lax.ppermute(block, axis, [(i, (i + shift) % count) for i in range(count)]))
    return jnp.stack(parts)


def scatter_slots(partial, axis):
    count = lax.axis_size(axis)
    total = partial[0].astype(jnp.float32)
    for shift in range(1, count):
        total = total + lax.ppermute(
            partial[shift], axis, [((i + shift) % count, i) for i in range(count)]
        ).astype(jnp.float32)
    return total


def send_slots(block, axis):
    count = lax.axis_size(axis)
    parts = [block]
    for shift in range(1, count):
        parts.append(lax.ppermute(block, axis, [(i, (i + shift) % count) for i in range(count)]))
    return parts


def attention_kernel(query_ref, *refs):
    *pair_refs, mask_ref, out_ref = refs
    query = query_ref[...]
    numerator = None
    denominator = None
    for block, pair_ref in enumerate(pair_refs):
        pairs = pair_ref[...]
        scores = lax.dot_general(
            query, pairs, (((1,), (1,)), ((), ())), preferred_element_type=jnp.float32
        ) * (1.0 / math.sqrt(HD))
        weights = jnp.exp(scores) * mask_ref[block]
        part_den = jnp.sum(weights, axis=1, keepdims=True)
        part_num = jnp.dot(weights.astype(jnp.bfloat16), pairs, preferred_element_type=jnp.float32)
        numerator = part_num if numerator is None else numerator + part_num
        denominator = part_den if denominator is None else denominator + part_den
    out_ref[...] = (numerator / denominator).astype(out_ref.dtype)


def attend(query_rows, pair_blocks, usable, heads, tile):
    requests, rows, lanes = query_rows.shape
    keys = pair_blocks[0].shape[0] // requests
    return pl.pallas_call(
        attention_kernel,
        grid=(requests, heads),
        in_specs=[pl.BlockSpec((None, rows, tile), lambda r, h: (r, 0, h))]
        + [pl.BlockSpec((keys, tile), lambda r, h: (r, h)) for _ in pair_blocks]
        + [pl.BlockSpec((None, len(pair_blocks), 1, keys), lambda r, h: (r, 0, 0, 0))],
        out_specs=pl.BlockSpec((None, rows, tile), lambda r, h: (r, 0, h)),
        out_shape=jax.ShapeDtypeStruct((requests, rows, lanes), jnp.bfloat16),
    )(query_rows, *pair_blocks, usable)


def per_request(vector, values, axis):
    shape = [1] * values.ndim
    shape[axis] = vector.shape[0]
    shape[-1] = vector.shape[-1]
    return vector.reshape(shape)


def modulate(values, shift, scale, axis):
    average = jnp.mean(values, -1, keepdims=True)
    centred = values - average
    spread = jnp.mean(centred * centred, -1, keepdims=True)
    normed = centred * lax.rsqrt(spread + 1e-06)
    return normed * (1.0 + per_request(scale, values, axis)) + per_request(shift, values, axis)


def head_norm(values, gain):
    width = values.shape[-1]
    lane_head = jnp.arange(width) // HD
    spread = (lane_head[:, None] == lane_head[None, :]).astype(jnp.float32) / HD
    mean_square = jnp.dot(values * values, spread, precision=lax.Precision.HIGHEST)
    return (values * lax.rsqrt(mean_square + 1e-06) * jnp.tile(gain, width // HD)).astype(jnp.bfloat16)


def noise_level(fraction):
    return 3.0 * fraction / (1.0 + 2.0 * fraction)


def attention_inputs(normed, weight, gains):
    model_width, _, local_width = weight.shape
    heads = local_width // HD
    split = weight.reshape(model_width, 3, heads, HD)
    query_weight = jnp.concatenate([split[:, 0], jnp.zeros_like(split[:, 0])], -1).reshape(
        model_width, 2 * local_width
    )
    pair_weight = jnp.concatenate([split[:, 1], split[:, 2]], -1).reshape(model_width, 2 * local_width)
    lane = jnp.arange(2 * local_width)
    live = (lane % (2 * HD)) < HD
    lane_head = lane // (2 * HD)
    spread = ((lane_head[:, None] == lane_head[None, :]) & live[:, None]).astype(jnp.float32) / HD
    query_gain = jnp.where(live, jnp.tile(jnp.concatenate([gains[0], gains[0]]), heads), 0.0)
    key_gain = jnp.tile(jnp.concatenate([gains[1], gains[1]]), heads)

    def normalized(values, gain):
        mean_square = jnp.dot(values * values, spread, precision=lax.Precision.HIGHEST)
        return values * lax.rsqrt(mean_square + 1e-06) * gain

    query_proj = jnp.einsum("arnd,de->arne", normed, query_weight, preferred_element_type=jnp.float32)
    pair_proj = jnp.einsum("arnd,de->arne", normed, pair_weight, preferred_element_type=jnp.float32)
    queries = normalized(query_proj, query_gain).astype(jnp.bfloat16)
    pairs = jnp.where(live, normalized(pair_proj, key_gain), pair_proj).astype(jnp.bfloat16)
    return queries, pairs


def convolve(padded, kernel):
    out_rows = padded.shape[1] - 2
    out_cols = padded.shape[2] - 2
    taps = jnp.concatenate(
        [
            padded[:, row_off : row_off + out_rows, col_off : col_off + out_cols]
            for row_off in range(3)
            for col_off in range(3)
        ],
        -1,
    )
    flat_kernel = kernel.reshape(-1, kernel.shape[-1])
    summed = jnp.einsum("rhwc,co->rhwo", taps, flat_kernel, preferred_element_type=jnp.float32)
    return summed.astype(jnp.bfloat16)


def body(
    image_hidden,
    text_hidden,
    latent_grid,
    text_lengths,
    step_index,
    image_mod,
    text_mod,
    final_mod,
    image_qk_gain,
    text_qk_gain,
    image_qkv,
    text_qkv,
    image_proj,
    text_proj,
    image_up,
    text_up,
    image_down,
    text_down,
    final_proj,
    conv_kernel,
):
    blocks = lax.axis_size("blk")
    groups = lax.axis_size("head")
    requests, tile_rows, tile_cols, model_width = image_hidden.shape
    text_slice = text_hidden.shape[1]
    image_tile = tile_rows * tile_cols
    tile_tokens = image_tile + text_slice
    own = jnp.concatenate(
        [image_hidden.reshape(requests, image_tile, model_width), text_hidden], axis=1
    )
    strip = gather_slots(own, "head")
    strip_f = strip.astype(jnp.float32)
    image_x = strip_f[:, :, :image_tile]
    text_x = strip_f[:, :, image_tile:]
    image_norm = modulate(image_x, image_mod[:, 0], image_mod[:, 1], 1).astype(jnp.bfloat16)
    text_norm = modulate(text_x, text_mod[:, 0], text_mod[:, 1], 1).astype(jnp.bfloat16)
    image_q, image_kv = attention_inputs(image_norm, image_qkv, image_qk_gain)
    text_q, text_kv = attention_inputs(text_norm, text_qkv, text_qk_gain)
    queries = jnp.concatenate([image_q, text_q], 2)
    key_value = jnp.concatenate([image_kv, text_kv], 2)
    tile = 2 * HD
    local_heads = queries.shape[-1] // tile
    local_width = local_heads * HD
    score_scale = 1.0 / math.sqrt(HD)
    own_pairs = key_value.transpose(1, 0, 2, 3).reshape(-1, local_heads * tile)
    flip_core = [(j, j ^ 1) for j in range(blocks)]
    flip_chip = [(j, j ^ 2) for j in range(blocks)]
    far = lax.ppermute(own_pairs, "blk", flip_chip)
    pair_blocks = [
        own_pairs,
        lax.ppermute(own_pairs, "blk", flip_core),
        far,
        lax.ppermute(far, "blk", flip_core),
    ]
    query_rows = groups * tile_tokens
    query_piece = queries.transpose(1, 0, 2, 3).reshape(requests, query_rows, local_heads * tile)
    position = jnp.arange(query_rows, dtype=jnp.int32)
    group = (lax.axis_index("head") - position // tile_tokens) % groups
    within = position % tile_tokens
    source = jnp.bitwise_xor(lax.axis_index("blk"), jnp.arange(blocks, dtype=jnp.int32))
    slot_ids = (group[None, :] * blocks + source[:, None]) * text_slice + (within - image_tile)[None, :]
    usable = (within < image_tile)[None, None, :] | (
        slot_ids[None, :, :] < text_lengths[:, None, None]
    )
    usable = usable.astype(jnp.float32).reshape(requests, blocks, 1, query_rows)
    attended = attend(query_piece, pair_blocks, usable, local_heads, tile)
    context = attended.reshape(requests, groups, tile_tokens, local_heads * tile)

    def padded_rows(weight):
        shaped = weight.reshape(local_heads, HD, weight.shape[-1])
        return jnp.concatenate([jnp.zeros_like(shaped), shaped], 1).reshape(local_heads * tile, -1)

    image_part = jnp.einsum(
        "rane,ed->arnd", context[:, :, :image_tile], padded_rows(image_proj), preferred_element_type=jnp.float32
    )
    text_part = jnp.einsum(
        "rane,ed->arnd", context[:, :, image_tile:], padded_rows(text_proj), preferred_element_type=jnp.float32
    )
    attn = scatter_slots(jnp.concatenate([image_part, text_part], 2).astype(jnp.bfloat16), "head")
    own_f = own.astype(jnp.float32)
    image_mid = own_f[:, :image_tile] + per_request(image_mod[:, 2], own_f, 0) * attn[:, :image_tile]
    text_mid = own_f[:, image_tile:] + per_request(text_mod[:, 2], own_f, 0) * attn[:, image_tile:]
    image_local = modulate(image_mid, image_mod[:, 3], image_mod[:, 4], 0).astype(jnp.bfloat16)
    text_local = modulate(text_mid, text_mod[:, 3], text_mod[:, 4], 0).astype(jnp.bfloat16)
    ff_in = gather_slots(jnp.concatenate([image_local, text_local], 1), "head")
    image_hid = jax.nn.gelu(
        jnp.einsum("arnd,df->arnf", ff_in[:, :, :image_tile], image_up, preferred_element_type=jnp.float32),
        approximate=True,
    ).astype(jnp.bfloat16)
    text_hid = jax.nn.gelu(
        jnp.einsum("arnd,df->arnf", ff_in[:, :, image_tile:], text_up, preferred_element_type=jnp.float32),
        approximate=True,
    ).astype(jnp.bfloat16)
    image_back = jnp.einsum("arnf,fd->arnd", image_hid, image_down, preferred_element_type=jnp.float32)
    text_back = jnp.einsum("arnf,fd->arnd", text_hid, text_down, preferred_element_type=jnp.float32)
    mlp = scatter_slots(jnp.concatenate([image_back, text_back], 2).astype(jnp.bfloat16), "head")
    image_out = image_mid + per_request(image_mod[:, 5], image_mid, 0) * mlp[:, :image_tile]
    text_out = text_mid + per_request(text_mod[:, 5], text_mid, 0) * mlp[:, image_tile:]
    image_states = image_out.reshape(requests, tile_rows, tile_cols, model_width).astype(jnp.bfloat16)
    text_states = text_out.astype(jnp.bfloat16)
    final_in = modulate(image_out, final_mod[:, 1], final_mod[:, 0], 0).astype(jnp.bfloat16)
    velocity = jnp.einsum("rnd,dp->rnp", final_in, final_proj, preferred_element_type=jnp.float32)
    channels = velocity.shape[-1] // 4
    velocity = (
        velocity.reshape(requests, tile_rows, tile_cols, 2, 2, channels)
        .transpose(0, 1, 3, 2, 4, 5)
        .reshape(requests, 2 * tile_rows, 2 * tile_cols, channels)
    )
    current = step_index.astype(jnp.float32) / 1000.0
    following = jnp.maximum(step_index - 125, 0).astype(jnp.float32) / 1000.0
    step_size = noise_level(following) - noise_level(current)
    latent_next = latent_grid + step_size[:, None, None, None] * velocity
    decoded_in = (latent_next / 1.5305 + 0.0609).astype(jnp.bfloat16)
    padded = extended(decoded_in, (("head", 1), ("blk", 2)), 1)
    features = convolve(padded, conv_kernel)
    return (image_states, text_states, latent_next, features)


def solution(mesh):
    in_specs = (
        P("req", "head", "blk", None),
        P("req", ("head", "blk"), None),
        P("req", "head", "blk", None),
        P("req"),
        P("req"),
        P("req", None, None),
        P("req", None, None),
        P("req", None, None),
        P(),
        P(),
        P(None, None, "head"),
        P(None, None, "head"),
        P("head", None),
        P("head", None),
        P(None, "head"),
        P(None, "head"),
        P("head", None),
        P("head", None),
        P(),
        P(),
    )
    out_specs = (
        P("req", "head", "blk", None),
        P("req", ("head", "blk"), None),
        P("req", "head", "blk", None),
        P("req", "head", "blk", None),
    )
    return jax.shard_map(body, mesh=mesh, in_specs=in_specs, out_specs=out_specs, check_vma=False)
```

```python
import math

import jax
import jax.numpy as jnp
from jax import lax
from jax.experimental import pallas as pl
from jax.sharding import PartitionSpec as P

HD = 64


def extended(block, sides, width):
    for axis, dim in sides:
        count = lax.axis_size(axis)
        forward = [(i, i + 1) for i in range(count - 1)]
        backward = [(target, source) for source, target in forward]
        low = lax.ppermute(
            lax.slice_in_dim(block, block.shape[dim] - width, None, axis=dim), axis, forward
        )
        high = lax.ppermute(lax.slice_in_dim(block, 0, width, axis=dim), axis, backward)
        block = jnp.concatenate([low, block, high], axis=dim)
    return block


def moved(block, axis, shift):
    count = lax.axis_size(axis)
    if count == 8 and shift == count // 2:
        step = [(i, (i + count - 2) % count) for i in range(count)]
        return lax.ppermute(lax.ppermute(block, axis, step), axis, step)
    return lax.ppermute(block, axis, [(i, (i + shift) % count) for i in range(count)])


def gather_slots(block, axis):
    count = lax.axis_size(axis)
    parts = [block]
    for shift in range(1, count):
        parts.append(moved(block, axis, shift))
    return jnp.stack(parts)


def scatter_slots(partial, axis):
    count = lax.axis_size(axis)
    total = partial[0].astype(jnp.float32)
    for shift in range(1, count):
        total = total + moved(partial[shift], axis, count - shift).astype(jnp.float32)
    return total


def send_slots(block, axis):
    count = lax.axis_size(axis)
    parts = [block]
    for shift in range(1, count):
        parts.append(lax.ppermute(block, axis, [(i, (i + shift) % count) for i in range(count)]))
    return parts


def attention_kernel(query_ref, *refs):
    *pair_refs, mask_ref, out_ref = refs
    query = query_ref[...]
    numerator = None
    denominator = None
    for block, pair_ref in enumerate(pair_refs):
        pairs = pair_ref[...]
        scores = lax.dot_general(
            query, pairs, (((1,), (1,)), ((), ())), preferred_element_type=jnp.float32
        ) * (1.0 / math.sqrt(HD))
        weights = jnp.exp(scores) * mask_ref[block]
        part_den = jnp.sum(weights, axis=1, keepdims=True)
        part_num = jnp.dot(weights.astype(jnp.bfloat16), pairs, preferred_element_type=jnp.float32)
        numerator = part_num if numerator is None else numerator + part_num
        denominator = part_den if denominator is None else denominator + part_den
    out_ref[...] = (numerator / denominator).astype(out_ref.dtype)


def attend(query_rows, pair_blocks, usable, heads, tile):
    requests, rows, lanes = query_rows.shape
    keys = pair_blocks[0].shape[0] // requests
    return pl.pallas_call(
        attention_kernel,
        grid=(requests, heads),
        in_specs=[pl.BlockSpec((None, rows, tile), lambda r, h: (r, 0, h))]
        + [pl.BlockSpec((keys, tile), lambda r, h: (r, h)) for _ in pair_blocks]
        + [pl.BlockSpec((None, len(pair_blocks), 1, keys), lambda r, h: (r, 0, 0, 0))],
        out_specs=pl.BlockSpec((None, rows, tile), lambda r, h: (r, 0, h)),
        out_shape=jax.ShapeDtypeStruct((requests, rows, lanes), jnp.bfloat16),
    )(query_rows, *pair_blocks, usable)


def per_request(vector, values, axis):
    shape = [1] * values.ndim
    shape[axis] = vector.shape[0]
    shape[-1] = vector.shape[-1]
    return vector.reshape(shape)


def modulate(values, shift, scale, axis):
    average = jnp.mean(values, -1, keepdims=True)
    centred = values - average
    spread = jnp.mean(centred * centred, -1, keepdims=True)
    normed = centred * lax.rsqrt(spread + 1e-06)
    return normed * (1.0 + per_request(scale, values, axis)) + per_request(shift, values, axis)


def head_norm(values, gain):
    width = values.shape[-1]
    lane_head = jnp.arange(width) // HD
    spread = (lane_head[:, None] == lane_head[None, :]).astype(jnp.float32) / HD
    mean_square = jnp.dot(values * values, spread, precision=lax.Precision.HIGHEST)
    return (values * lax.rsqrt(mean_square + 1e-06) * jnp.tile(gain, width // HD)).astype(jnp.bfloat16)


def noise_level(fraction):
    return 3.0 * fraction / (1.0 + 2.0 * fraction)


def attention_inputs(normed, weight, gains):
    model_width, _, local_width = weight.shape
    heads = local_width // HD
    split = weight.reshape(model_width, 3, heads, HD)
    query_weight = jnp.concatenate([split[:, 0], jnp.zeros_like(split[:, 0])], -1).reshape(
        model_width, 2 * local_width
    )
    pair_weight = jnp.concatenate([split[:, 1], split[:, 2]], -1).reshape(model_width, 2 * local_width)
    lane = jnp.arange(2 * local_width)
    live = (lane % (2 * HD)) < HD
    lane_head = lane // (2 * HD)
    spread = ((lane_head[:, None] == lane_head[None, :]) & live[:, None]).astype(jnp.float32) / HD
    query_gain = jnp.where(live, jnp.tile(jnp.concatenate([gains[0], gains[0]]), heads), 0.0)
    key_gain = jnp.tile(jnp.concatenate([gains[1], gains[1]]), heads)

    def normalized(values, gain):
        mean_square = jnp.dot(values * values, spread, precision=lax.Precision.HIGHEST)
        return values * lax.rsqrt(mean_square + 1e-06) * gain

    query_proj = jnp.einsum("arnd,de->arne", normed, query_weight, preferred_element_type=jnp.float32)
    pair_proj = jnp.einsum("arnd,de->arne", normed, pair_weight, preferred_element_type=jnp.float32)
    queries = normalized(query_proj, query_gain).astype(jnp.bfloat16)
    pairs = jnp.where(live, normalized(pair_proj, key_gain), pair_proj).astype(jnp.bfloat16)
    return queries, pairs


def convolve(padded, kernel):
    out_rows = padded.shape[1] - 2
    out_cols = padded.shape[2] - 2
    summed = jnp.zeros((padded.shape[0], out_rows, out_cols, kernel.shape[-1]), jnp.float32)
    for row_off in range(3):
        for col_off in range(3):
            summed = summed + jnp.einsum(
                "rhwc,co->rhwo",
                padded[:, row_off : row_off + out_rows, col_off : col_off + out_cols],
                kernel[row_off, col_off],
                preferred_element_type=jnp.float32,
            )
    return summed.astype(jnp.bfloat16)


def body(
    image_hidden,
    text_hidden,
    latent_grid,
    text_lengths,
    step_index,
    image_mod,
    text_mod,
    final_mod,
    image_qk_gain,
    text_qk_gain,
    image_qkv,
    text_qkv,
    image_proj,
    text_proj,
    image_up,
    text_up,
    image_down,
    text_down,
    final_proj,
    conv_kernel,
):
    blocks = lax.axis_size("blk")
    groups = lax.axis_size("head")
    requests, tile_rows, tile_cols, model_width = image_hidden.shape
    text_slice = text_hidden.shape[1]
    image_tile = tile_rows * tile_cols
    tile_tokens = image_tile + text_slice
    own = jnp.concatenate(
        [image_hidden.reshape(requests, image_tile, model_width), text_hidden], axis=1
    )
    strip = gather_slots(own, "head")
    strip_f = strip.astype(jnp.float32)
    image_x = strip_f[:, :, :image_tile]
    text_x = strip_f[:, :, image_tile:]
    image_norm = modulate(image_x, image_mod[:, 0], image_mod[:, 1], 1).astype(jnp.bfloat16)
    text_norm = modulate(text_x, text_mod[:, 0], text_mod[:, 1], 1).astype(jnp.bfloat16)
    image_q, image_kv = attention_inputs(image_norm, image_qkv, image_qk_gain)
    text_q, text_kv = attention_inputs(text_norm, text_qkv, text_qk_gain)
    queries = jnp.concatenate([image_q, text_q], 2)
    key_value = jnp.concatenate([image_kv, text_kv], 2)
    tile = 2 * HD
    local_heads = queries.shape[-1] // tile
    local_width = local_heads * HD
    score_scale = 1.0 / math.sqrt(HD)
    own_pairs = key_value.transpose(1, 0, 2, 3).reshape(-1, local_heads * tile)
    flip_core = [(j, j ^ 1) for j in range(blocks)]
    flip_chip = [(j, j ^ 2) for j in range(blocks)]
    far = lax.ppermute(own_pairs, "blk", flip_chip)
    pair_blocks = [
        own_pairs,
        lax.ppermute(own_pairs, "blk", flip_core),
        far,
        lax.ppermute(far, "blk", flip_core),
    ]
    query_rows = groups * tile_tokens
    query_piece = queries.transpose(1, 0, 2, 3).reshape(requests, query_rows, local_heads * tile)
    position = jnp.arange(query_rows, dtype=jnp.int32)
    group = (lax.axis_index("head") - position // tile_tokens) % groups
    within = position % tile_tokens
    source = jnp.bitwise_xor(lax.axis_index("blk"), jnp.arange(blocks, dtype=jnp.int32))
    slot_ids = (group[None, :] * blocks + source[:, None]) * text_slice + (within - image_tile)[None, :]
    usable = (within < image_tile)[None, None, :] | (
        slot_ids[None, :, :] < text_lengths[:, None, None]
    )
    usable = usable.astype(jnp.float32).reshape(requests, blocks, 1, query_rows)
    attended = attend(query_piece, pair_blocks, usable, local_heads, tile)
    context = attended.reshape(requests, groups, tile_tokens, local_heads * tile)

    def padded_rows(weight):
        shaped = weight.reshape(local_heads, HD, weight.shape[-1])
        return jnp.concatenate([jnp.zeros_like(shaped), shaped], 1).reshape(local_heads * tile, -1)

    image_part = jnp.einsum(
        "rane,ed->arnd", context[:, :, :image_tile], padded_rows(image_proj), preferred_element_type=jnp.float32
    )
    text_part = jnp.einsum(
        "rane,ed->arnd", context[:, :, image_tile:], padded_rows(text_proj), preferred_element_type=jnp.float32
    )
    attn = scatter_slots(jnp.concatenate([image_part, text_part], 2).astype(jnp.bfloat16), "head")
    own_f = own.astype(jnp.float32)
    image_mid = own_f[:, :image_tile] + per_request(image_mod[:, 2], own_f, 0) * attn[:, :image_tile]
    text_mid = own_f[:, image_tile:] + per_request(text_mod[:, 2], own_f, 0) * attn[:, image_tile:]
    image_local = modulate(image_mid, image_mod[:, 3], image_mod[:, 4], 0).astype(jnp.bfloat16)
    text_local = modulate(text_mid, text_mod[:, 3], text_mod[:, 4], 0).astype(jnp.bfloat16)
    ff_in = gather_slots(jnp.concatenate([image_local, text_local], 1), "head")
    image_hid = jax.nn.gelu(
        jnp.einsum("arnd,df->arnf", ff_in[:, :, :image_tile], image_up, preferred_element_type=jnp.float32),
        approximate=True,
    ).astype(jnp.bfloat16)
    text_hid = jax.nn.gelu(
        jnp.einsum("arnd,df->arnf", ff_in[:, :, image_tile:], text_up, preferred_element_type=jnp.float32),
        approximate=True,
    ).astype(jnp.bfloat16)
    image_back = jnp.einsum("arnf,fd->arnd", image_hid, image_down, preferred_element_type=jnp.float32)
    text_back = jnp.einsum("arnf,fd->arnd", text_hid, text_down, preferred_element_type=jnp.float32)
    mlp = scatter_slots(jnp.concatenate([image_back, text_back], 2).astype(jnp.bfloat16), "head")
    image_out = image_mid + per_request(image_mod[:, 5], image_mid, 0) * mlp[:, :image_tile]
    text_out = text_mid + per_request(text_mod[:, 5], text_mid, 0) * mlp[:, image_tile:]
    image_states = image_out.reshape(requests, tile_rows, tile_cols, model_width).astype(jnp.bfloat16)
    text_states = text_out.astype(jnp.bfloat16)
    final_in = modulate(image_out, final_mod[:, 1], final_mod[:, 0], 0).astype(jnp.bfloat16)
    velocity = jnp.einsum("rnd,dp->rnp", final_in, final_proj, preferred_element_type=jnp.float32)
    channels = velocity.shape[-1] // 4
    velocity = (
        velocity.reshape(requests, tile_rows, tile_cols, 2, 2, channels)
        .transpose(0, 1, 3, 2, 4, 5)
        .reshape(requests, 2 * tile_rows, 2 * tile_cols, channels)
    )
    current = step_index.astype(jnp.float32) / 1000.0
    following = jnp.maximum(step_index - 125, 0).astype(jnp.float32) / 1000.0
    step_size = noise_level(following) - noise_level(current)
    latent_next = latent_grid + step_size[:, None, None, None] * velocity
    decoded_in = (latent_next / 1.5305 + 0.0609).astype(jnp.bfloat16)
    padded = extended(decoded_in, (("head", 1), ("blk", 2)), 1)
    features = convolve(padded, conv_kernel)
    return (image_states, text_states, latent_next, features)


def solution(mesh):
    in_specs = (
        P("req", "head", "blk", None),
        P("req", ("head", "blk"), None),
        P("req", "head", "blk", None),
        P("req"),
        P("req"),
        P("req", None, None),
        P("req", None, None),
        P("req", None, None),
        P(),
        P(),
        P(None, None, "head"),
        P(None, None, "head"),
        P("head", None),
        P("head", None),
        P(None, "head"),
        P(None, "head"),
        P("head", None),
        P("head", None),
        P(),
        P(),
    )
    out_specs = (
        P("req", "head", "blk", None),
        P("req", ("head", "blk"), None),
        P("req", "head", "blk", None),
        P("req", "head", "blk", None),
    )
    return jax.shard_map(body, mesh=mesh, in_specs=in_specs, out_specs=out_specs, check_vma=False)
```

```python
import math

import jax
import jax.numpy as jnp
from jax import lax
from jax.experimental import pallas as pl
from jax.sharding import PartitionSpec as P

HD = 64


def extended(block, sides, width):
    for axis, dim in sides:
        count = lax.axis_size(axis)
        forward = [(i, i + 1) for i in range(count - 1)]
        backward = [(target, source) for source, target in forward]
        low = lax.ppermute(
            lax.slice_in_dim(block, block.shape[dim] - width, None, axis=dim), axis, forward
        )
        high = lax.ppermute(lax.slice_in_dim(block, 0, width, axis=dim), axis, backward)
        block = jnp.concatenate([low, block, high], axis=dim)
    return block


def moved(block, axis, shift):
    count = lax.axis_size(axis)
    if count == 8 and shift == count // 2:
        step = [(i, (i + count - 2) % count) for i in range(count)]
        return lax.ppermute(lax.ppermute(block, axis, step), axis, step)
    return lax.ppermute(block, axis, [(i, (i + shift) % count) for i in range(count)])


def bordered(block):
    rows = lax.axis_size("head")
    cols = lax.axis_size("blk")

    def along(piece, axis, count, step):
        pairs = [(i, i + step) for i in range(count) if 0 <= i + step < count]
        return lax.ppermute(piece, axis, pairs)

    def diagonal(piece, row_step, col_step):
        pairs = [
            (i * cols + j, (i + row_step) * cols + j + col_step)
            for i in range(rows)
            for j in range(cols)
            if 0 <= i + row_step < rows and 0 <= j + col_step < cols
        ]
        return lax.ppermute(piece, ("head", "blk"), pairs)

    above = along(block[:, -1:], "head", rows, 1)
    below = along(block[:, :1], "head", rows, -1)
    left = along(block[:, :, -1:], "blk", cols, 1)
    right = along(block[:, :, :1], "blk", cols, -1)
    above_left = diagonal(block[:, -1:, -1:], 1, 1)
    above_right = diagonal(block[:, -1:, :1], 1, -1)
    below_left = diagonal(block[:, :1, -1:], -1, 1)
    below_right = diagonal(block[:, :1, :1], -1, -1)
    top = jnp.concatenate([above_left, above, above_right], 2)
    middle = jnp.concatenate([left, block, right], 2)
    bottom = jnp.concatenate([below_left, below, below_right], 2)
    return jnp.concatenate([top, middle, bottom], 1)


def gather_slots(block, axis):
    count = lax.axis_size(axis)
    parts = [block]
    for shift in range(1, count):
        parts.append(moved(block, axis, shift))
    return jnp.stack(parts)


def scatter_slots(partial, axis):
    count = lax.axis_size(axis)
    total = partial[0].astype(jnp.float32)
    for shift in range(1, count):
        total = total + moved(partial[shift], axis, count - shift).astype(jnp.float32)
    return total


def send_slots(block, axis):
    count = lax.axis_size(axis)
    parts = [block]
    for shift in range(1, count):
        parts.append(lax.ppermute(block, axis, [(i, (i + shift) % count) for i in range(count)]))
    return parts


def attention_kernel(query_ref, *refs):
    *pair_refs, mask_ref, out_ref = refs
    query = query_ref[...]
    numerator = None
    denominator = None
    for block, pair_ref in enumerate(pair_refs):
        pairs = pair_ref[...]
        scores = lax.dot_general(
            query, pairs, (((1,), (1,)), ((), ())), preferred_element_type=jnp.float32
        ) * (1.0 / math.sqrt(HD))
        weights = jnp.exp(scores) * mask_ref[block]
        part_den = jnp.sum(weights, axis=1, keepdims=True)
        part_num = jnp.dot(weights.astype(jnp.bfloat16), pairs, preferred_element_type=jnp.float32)
        numerator = part_num if numerator is None else numerator + part_num
        denominator = part_den if denominator is None else denominator + part_den
    out_ref[...] = (numerator / denominator).astype(out_ref.dtype)


def attend(query_rows, pair_blocks, usable, heads, tile):
    requests, rows, lanes = query_rows.shape
    keys = pair_blocks[0].shape[0] // requests
    return pl.pallas_call(
        attention_kernel,
        grid=(requests, heads),
        in_specs=[pl.BlockSpec((None, rows, tile), lambda r, h: (r, 0, h))]
        + [pl.BlockSpec((keys, tile), lambda r, h: (r, h)) for _ in pair_blocks]
        + [pl.BlockSpec((None, len(pair_blocks), 1, keys), lambda r, h: (r, 0, 0, 0))],
        out_specs=pl.BlockSpec((None, rows, tile), lambda r, h: (r, 0, h)),
        out_shape=jax.ShapeDtypeStruct((requests, rows, lanes), jnp.bfloat16),
    )(query_rows, *pair_blocks, usable)


def per_request(vector, values, axis):
    shape = [1] * values.ndim
    shape[axis] = vector.shape[0]
    shape[-1] = vector.shape[-1]
    return vector.reshape(shape)


def modulate(values, shift, scale, axis):
    average = jnp.mean(values, -1, keepdims=True)
    centred = values - average
    spread = jnp.mean(centred * centred, -1, keepdims=True)
    normed = centred * lax.rsqrt(spread + 1e-06)
    return normed * (1.0 + per_request(scale, values, axis)) + per_request(shift, values, axis)


def head_norm(values, gain):
    width = values.shape[-1]
    lane_head = jnp.arange(width) // HD
    spread = (lane_head[:, None] == lane_head[None, :]).astype(jnp.float32) / HD
    mean_square = jnp.dot(values * values, spread, precision=lax.Precision.HIGHEST)
    return (values * lax.rsqrt(mean_square + 1e-06) * jnp.tile(gain, width // HD)).astype(jnp.bfloat16)


def noise_level(fraction):
    return 3.0 * fraction / (1.0 + 2.0 * fraction)


def attention_inputs(normed, weight, gains):
    model_width, _, local_width = weight.shape
    heads = local_width // HD
    split = weight.reshape(model_width, 3, heads, HD)
    query_weight = jnp.concatenate([split[:, 0], jnp.zeros_like(split[:, 0])], -1).reshape(
        model_width, 2 * local_width
    )
    pair_weight = jnp.concatenate([split[:, 1], split[:, 2]], -1).reshape(model_width, 2 * local_width)
    lane = jnp.arange(2 * local_width)
    live = (lane % (2 * HD)) < HD
    lane_head = lane // (2 * HD)
    spread = ((lane_head[:, None] == lane_head[None, :]) & live[:, None]).astype(jnp.float32) / HD
    query_gain = jnp.where(live, jnp.tile(jnp.concatenate([gains[0], gains[0]]), heads), 0.0)
    key_gain = jnp.tile(jnp.concatenate([gains[1], gains[1]]), heads)

    def normalized(values, gain):
        mean_square = jnp.dot(values * values, spread, precision=lax.Precision.HIGHEST)
        return values * lax.rsqrt(mean_square + 1e-06) * gain

    query_proj = jnp.einsum("arnd,de->arne", normed, query_weight, preferred_element_type=jnp.float32)
    pair_proj = jnp.einsum("arnd,de->arne", normed, pair_weight, preferred_element_type=jnp.float32)
    queries = normalized(query_proj, query_gain).astype(jnp.bfloat16)
    pairs = jnp.where(live, normalized(pair_proj, key_gain), pair_proj).astype(jnp.bfloat16)
    return queries, pairs


def convolve(padded, kernel):
    out_rows = padded.shape[1] - 2
    out_cols = padded.shape[2] - 2
    summed = jnp.zeros((padded.shape[0], out_rows, out_cols, kernel.shape[-1]), jnp.float32)
    for row_off in range(3):
        for col_off in range(3):
            summed = summed + jnp.einsum(
                "rhwc,co->rhwo",
                padded[:, row_off : row_off + out_rows, col_off : col_off + out_cols],
                kernel[row_off, col_off],
                preferred_element_type=jnp.float32,
            )
    return summed.astype(jnp.bfloat16)


def body(
    image_hidden,
    text_hidden,
    latent_grid,
    text_lengths,
    step_index,
    image_mod,
    text_mod,
    final_mod,
    image_qk_gain,
    text_qk_gain,
    image_qkv,
    text_qkv,
    image_proj,
    text_proj,
    image_up,
    text_up,
    image_down,
    text_down,
    final_proj,
    conv_kernel,
):
    blocks = lax.axis_size("blk")
    groups = lax.axis_size("head")
    requests, tile_rows, tile_cols, model_width = image_hidden.shape
    text_slice = text_hidden.shape[1]
    image_tile = tile_rows * tile_cols
    tile_tokens = image_tile + text_slice
    own = jnp.concatenate(
        [image_hidden.reshape(requests, image_tile, model_width), text_hidden], axis=1
    )
    strip = gather_slots(own, "head")
    strip_f = strip.astype(jnp.float32)
    image_x = strip_f[:, :, :image_tile]
    text_x = strip_f[:, :, image_tile:]
    image_norm = modulate(image_x, image_mod[:, 0], image_mod[:, 1], 1).astype(jnp.bfloat16)
    text_norm = modulate(text_x, text_mod[:, 0], text_mod[:, 1], 1).astype(jnp.bfloat16)
    image_q, image_kv = attention_inputs(image_norm, image_qkv, image_qk_gain)
    text_q, text_kv = attention_inputs(text_norm, text_qkv, text_qk_gain)
    queries = jnp.concatenate([image_q, text_q], 2)
    key_value = jnp.concatenate([image_kv, text_kv], 2)
    tile = 2 * HD
    local_heads = queries.shape[-1] // tile
    local_width = local_heads * HD
    score_scale = 1.0 / math.sqrt(HD)
    own_pairs = key_value.transpose(1, 0, 2, 3).reshape(-1, local_heads * tile)
    flip_core = [(j, j ^ 1) for j in range(blocks)]
    flip_chip = [(j, j ^ 2) for j in range(blocks)]
    far = lax.ppermute(own_pairs, "blk", flip_chip)
    pair_blocks = [
        own_pairs,
        lax.ppermute(own_pairs, "blk", flip_core),
        far,
        lax.ppermute(far, "blk", flip_core),
    ]
    query_rows = groups * tile_tokens
    query_piece = queries.transpose(1, 0, 2, 3).reshape(requests, query_rows, local_heads * tile)
    position = jnp.arange(query_rows, dtype=jnp.int32)
    group = (lax.axis_index("head") - position // tile_tokens) % groups
    within = position % tile_tokens
    source = jnp.bitwise_xor(lax.axis_index("blk"), jnp.arange(blocks, dtype=jnp.int32))
    slot_ids = (group[None, :] * blocks + source[:, None]) * text_slice + (within - image_tile)[None, :]
    usable = (within < image_tile)[None, None, :] | (
        slot_ids[None, :, :] < text_lengths[:, None, None]
    )
    usable = usable.astype(jnp.float32).reshape(requests, blocks, 1, query_rows)
    attended = attend(query_piece, pair_blocks, usable, local_heads, tile)
    context = attended.reshape(requests, groups, tile_tokens, local_heads * tile)

    def padded_rows(weight):
        shaped = weight.reshape(local_heads, HD, weight.shape[-1])
        return jnp.concatenate([jnp.zeros_like(shaped), shaped], 1).reshape(local_heads * tile, -1)

    image_part = jnp.einsum(
        "rane,ed->arnd", context[:, :, :image_tile], padded_rows(image_proj), preferred_element_type=jnp.float32
    )
    text_part = jnp.einsum(
        "rane,ed->arnd", context[:, :, image_tile:], padded_rows(text_proj), preferred_element_type=jnp.float32
    )
    attn = scatter_slots(jnp.concatenate([image_part, text_part], 2).astype(jnp.bfloat16), "head")
    own_f = own.astype(jnp.float32)
    image_mid = own_f[:, :image_tile] + per_request(image_mod[:, 2], own_f, 0) * attn[:, :image_tile]
    text_mid = own_f[:, image_tile:] + per_request(text_mod[:, 2], own_f, 0) * attn[:, image_tile:]
    image_local = modulate(image_mid, image_mod[:, 3], image_mod[:, 4], 0).astype(jnp.bfloat16)
    text_local = modulate(text_mid, text_mod[:, 3], text_mod[:, 4], 0).astype(jnp.bfloat16)
    ff_in = gather_slots(jnp.concatenate([image_local, text_local], 1), "head")
    image_hid = jax.nn.gelu(
        jnp.einsum("arnd,df->arnf", ff_in[:, :, :image_tile], image_up, preferred_element_type=jnp.float32),
        approximate=True,
    ).astype(jnp.bfloat16)
    text_hid = jax.nn.gelu(
        jnp.einsum("arnd,df->arnf", ff_in[:, :, image_tile:], text_up, preferred_element_type=jnp.float32),
        approximate=True,
    ).astype(jnp.bfloat16)
    image_back = jnp.einsum("arnf,fd->arnd", image_hid, image_down, preferred_element_type=jnp.float32)
    text_back = jnp.einsum("arnf,fd->arnd", text_hid, text_down, preferred_element_type=jnp.float32)
    mlp = scatter_slots(jnp.concatenate([image_back, text_back], 2).astype(jnp.bfloat16), "head")
    image_out = image_mid + per_request(image_mod[:, 5], image_mid, 0) * mlp[:, :image_tile]
    text_out = text_mid + per_request(text_mod[:, 5], text_mid, 0) * mlp[:, image_tile:]
    image_states = image_out.reshape(requests, tile_rows, tile_cols, model_width).astype(jnp.bfloat16)
    text_states = text_out.astype(jnp.bfloat16)
    final_in = modulate(image_out, final_mod[:, 1], final_mod[:, 0], 0).astype(jnp.bfloat16)
    velocity = jnp.einsum("rnd,dp->rnp", final_in, final_proj, preferred_element_type=jnp.float32)
    channels = velocity.shape[-1] // 4
    velocity = (
        velocity.reshape(requests, tile_rows, tile_cols, 2, 2, channels)
        .transpose(0, 1, 3, 2, 4, 5)
        .reshape(requests, 2 * tile_rows, 2 * tile_cols, channels)
    )
    current = step_index.astype(jnp.float32) / 1000.0
    following = jnp.maximum(step_index - 125, 0).astype(jnp.float32) / 1000.0
    step_size = noise_level(following) - noise_level(current)
    latent_next = latent_grid + step_size[:, None, None, None] * velocity
    decoded_in = (latent_next / 1.5305 + 0.0609).astype(jnp.bfloat16)
    padded = bordered(decoded_in)
    features = convolve(padded, conv_kernel)
    return (image_states, text_states, latent_next, features)


def solution(mesh):
    in_specs = (
        P("req", "head", "blk", None),
        P("req", ("head", "blk"), None),
        P("req", "head", "blk", None),
        P("req"),
        P("req"),
        P("req", None, None),
        P("req", None, None),
        P("req", None, None),
        P(),
        P(),
        P(None, None, "head"),
        P(None, None, "head"),
        P("head", None),
        P("head", None),
        P(None, "head"),
        P(None, "head"),
        P("head", None),
        P("head", None),
        P(),
        P(),
    )
    out_specs = (
        P("req", "head", "blk", None),
        P("req", ("head", "blk"), None),
        P("req", "head", "blk", None),
        P("req", "head", "blk", None),
    )
    return jax.shard_map(body, mesh=mesh, in_specs=in_specs, out_specs=out_specs, check_vma=False)
```

```python
import math

import jax
import jax.numpy as jnp
from jax import lax
from jax.experimental import pallas as pl
from jax.sharding import PartitionSpec as P

HD = 64


def extended(block, sides, width):
    for axis, dim in sides:
        count = lax.axis_size(axis)
        forward = [(i, i + 1) for i in range(count - 1)]
        backward = [(target, source) for source, target in forward]
        low = lax.ppermute(
            lax.slice_in_dim(block, block.shape[dim] - width, None, axis=dim), axis, forward
        )
        high = lax.ppermute(lax.slice_in_dim(block, 0, width, axis=dim), axis, backward)
        block = jnp.concatenate([low, block, high], axis=dim)
    return block


def moved(block, axis, shift):
    count = lax.axis_size(axis)
    if count == 8 and shift == count // 2:
        step = [(i, (i + count - 2) % count) for i in range(count)]
        return lax.ppermute(lax.ppermute(block, axis, step), axis, step)
    return lax.ppermute(block, axis, [(i, (i + shift) % count) for i in range(count)])


def gather_slots(block, axis):
    count = lax.axis_size(axis)
    parts = [block]
    for shift in range(1, count):
        parts.append(moved(block, axis, shift))
    return jnp.stack(parts)


def scatter_slots(partial, axis):
    count = lax.axis_size(axis)
    total = partial[0].astype(jnp.float32)
    for shift in range(1, count):
        total = total + moved(partial[shift], axis, count - shift).astype(jnp.float32)
    return total


def send_slots(block, axis):
    count = lax.axis_size(axis)
    parts = [block]
    for shift in range(1, count):
        parts.append(lax.ppermute(block, axis, [(i, (i + shift) % count) for i in range(count)]))
    return parts


def attention_kernel(query_ref, *refs):
    *pair_refs, mask_ref, out_ref = refs
    query = query_ref[...]
    numerator = None
    denominator = None
    for block, pair_ref in enumerate(pair_refs):
        pairs = pair_ref[...]
        scores = lax.dot_general(
            query, pairs, (((1,), (1,)), ((), ())), preferred_element_type=jnp.float32
        ) * (1.0 / math.sqrt(HD))
        weights = jnp.exp(scores) * mask_ref[block]
        part_den = jnp.sum(weights, axis=1, keepdims=True)
        part_num = jnp.dot(weights.astype(jnp.bfloat16), pairs, preferred_element_type=jnp.float32)
        numerator = part_num if numerator is None else numerator + part_num
        denominator = part_den if denominator is None else denominator + part_den
    out_ref[...] = (numerator / denominator).astype(out_ref.dtype)


def attend(query_rows, pair_blocks, usable, heads, tile):
    requests, rows, lanes = query_rows.shape
    keys = pair_blocks[0].shape[0] // requests
    return pl.pallas_call(
        attention_kernel,
        grid=(requests, heads),
        in_specs=[pl.BlockSpec((None, rows, tile), lambda r, h: (r, 0, h))]
        + [pl.BlockSpec((keys, tile), lambda r, h: (r, h)) for _ in pair_blocks]
        + [pl.BlockSpec((None, len(pair_blocks), 1, keys), lambda r, h: (r, 0, 0, 0))],
        out_specs=pl.BlockSpec((None, rows, tile), lambda r, h: (r, 0, h)),
        out_shape=jax.ShapeDtypeStruct((requests, rows, lanes), jnp.bfloat16),
    )(query_rows, *pair_blocks, usable)


def per_request(vector, values, axis):
    shape = [1] * values.ndim
    shape[axis] = vector.shape[0]
    shape[-1] = vector.shape[-1]
    return vector.reshape(shape)


def modulate(values, shift, scale, axis):
    average = jnp.mean(values, -1, keepdims=True)
    centred = values - average
    spread = jnp.mean(centred * centred, -1, keepdims=True)
    normed = centred * lax.rsqrt(spread + 1e-06)
    return normed * (1.0 + per_request(scale, values, axis)) + per_request(shift, values, axis)


def head_norm(values, gain):
    width = values.shape[-1]
    lane_head = jnp.arange(width) // HD
    spread = (lane_head[:, None] == lane_head[None, :]).astype(jnp.float32) / HD
    mean_square = jnp.dot(values * values, spread, precision=lax.Precision.HIGH)
    return (values * lax.rsqrt(mean_square + 1e-06) * jnp.tile(gain, width // HD)).astype(jnp.bfloat16)


def noise_level(fraction):
    return 3.0 * fraction / (1.0 + 2.0 * fraction)


def attention_inputs(normed, weight, gains):
    model_width, _, local_width = weight.shape
    heads = local_width // HD
    split = weight.reshape(model_width, 3, heads, HD)
    query_weight = jnp.concatenate([split[:, 0], jnp.zeros_like(split[:, 0])], -1).reshape(
        model_width, 2 * local_width
    )
    pair_weight = jnp.concatenate([split[:, 1], split[:, 2]], -1).reshape(model_width, 2 * local_width)
    lane = jnp.arange(2 * local_width)
    live = (lane % (2 * HD)) < HD
    lane_head = lane // (2 * HD)
    spread = ((lane_head[:, None] == lane_head[None, :]) & live[:, None]).astype(jnp.float32) / HD
    query_gain = jnp.where(live, jnp.tile(jnp.concatenate([gains[0], gains[0]]), heads), 0.0)
    key_gain = jnp.tile(jnp.concatenate([gains[1], gains[1]]), heads)

    def normalized(values, gain):
        mean_square = jnp.dot(values * values, spread, precision=lax.Precision.HIGH)
        return values * lax.rsqrt(mean_square + 1e-06) * gain

    query_proj = jnp.einsum("arnd,de->arne", normed, query_weight, preferred_element_type=jnp.float32)
    pair_proj = jnp.einsum("arnd,de->arne", normed, pair_weight, preferred_element_type=jnp.float32)
    queries = normalized(query_proj, query_gain).astype(jnp.bfloat16)
    pairs = jnp.where(live, normalized(pair_proj, key_gain), pair_proj).astype(jnp.bfloat16)
    return queries, pairs


def convolve(padded, kernel):
    out_rows = padded.shape[1] - 2
    out_cols = padded.shape[2] - 2
    summed = jnp.zeros((padded.shape[0], out_rows, out_cols, kernel.shape[-1]), jnp.float32)
    for row_off in range(3):
        for col_off in range(3):
            summed = summed + jnp.einsum(
                "rhwc,co->rhwo",
                padded[:, row_off : row_off + out_rows, col_off : col_off + out_cols],
                kernel[row_off, col_off],
                preferred_element_type=jnp.float32,
            )
    return summed.astype(jnp.bfloat16)


def body(
    image_hidden,
    text_hidden,
    latent_grid,
    text_lengths,
    step_index,
    image_mod,
    text_mod,
    final_mod,
    image_qk_gain,
    text_qk_gain,
    image_qkv,
    text_qkv,
    image_proj,
    text_proj,
    image_up,
    text_up,
    image_down,
    text_down,
    final_proj,
    conv_kernel,
):
    blocks = lax.axis_size("blk")
    groups = lax.axis_size("head")
    requests, tile_rows, tile_cols, model_width = image_hidden.shape
    text_slice = text_hidden.shape[1]
    image_tile = tile_rows * tile_cols
    tile_tokens = image_tile + text_slice
    own = jnp.concatenate(
        [image_hidden.reshape(requests, image_tile, model_width), text_hidden], axis=1
    )
    strip = gather_slots(own, "head")
    strip_f = strip.astype(jnp.float32)
    image_x = strip_f[:, :, :image_tile]
    text_x = strip_f[:, :, image_tile:]
    image_norm = modulate(image_x, image_mod[:, 0], image_mod[:, 1], 1).astype(jnp.bfloat16)
    text_norm = modulate(text_x, text_mod[:, 0], text_mod[:, 1], 1).astype(jnp.bfloat16)
    image_q, image_kv = attention_inputs(image_norm, image_qkv, image_qk_gain)
    text_q, text_kv = attention_inputs(text_norm, text_qkv, text_qk_gain)
    queries = jnp.concatenate([image_q, text_q], 2)
    key_value = jnp.concatenate([image_kv, text_kv], 2)
    tile = 2 * HD
    local_heads = queries.shape[-1] // tile
    local_width = local_heads * HD
    score_scale = 1.0 / math.sqrt(HD)
    own_pairs = key_value.transpose(1, 0, 2, 3).reshape(-1, local_heads * tile)
    flip_core = [(j, j ^ 1) for j in range(blocks)]
    flip_chip = [(j, j ^ 2) for j in range(blocks)]
    far = lax.ppermute(own_pairs, "blk", flip_chip)
    pair_blocks = [
        own_pairs,
        lax.ppermute(own_pairs, "blk", flip_core),
        far,
        lax.ppermute(far, "blk", flip_core),
    ]
    query_rows = groups * tile_tokens
    query_piece = queries.transpose(1, 0, 2, 3).reshape(requests, query_rows, local_heads * tile)
    position = jnp.arange(query_rows, dtype=jnp.int32)
    group = (lax.axis_index("head") - position // tile_tokens) % groups
    within = position % tile_tokens
    source = jnp.bitwise_xor(lax.axis_index("blk"), jnp.arange(blocks, dtype=jnp.int32))
    slot_ids = (group[None, :] * blocks + source[:, None]) * text_slice + (within - image_tile)[None, :]
    usable = (within < image_tile)[None, None, :] | (
        slot_ids[None, :, :] < text_lengths[:, None, None]
    )
    usable = usable.astype(jnp.float32).reshape(requests, blocks, 1, query_rows)
    attended = attend(query_piece, pair_blocks, usable, local_heads, tile)
    context = attended.reshape(requests, groups, tile_tokens, local_heads * tile)

    def padded_rows(weight):
        shaped = weight.reshape(local_heads, HD, weight.shape[-1])
        return jnp.concatenate([jnp.zeros_like(shaped), shaped], 1).reshape(local_heads * tile, -1)

    image_part = jnp.einsum(
        "rane,ed->arnd", context[:, :, :image_tile], padded_rows(image_proj), preferred_element_type=jnp.float32
    )
    text_part = jnp.einsum(
        "rane,ed->arnd", context[:, :, image_tile:], padded_rows(text_proj), preferred_element_type=jnp.float32
    )
    attn = scatter_slots(jnp.concatenate([image_part, text_part], 2).astype(jnp.bfloat16), "head")
    own_f = own.astype(jnp.float32)
    image_mid = own_f[:, :image_tile] + per_request(image_mod[:, 2], own_f, 0) * attn[:, :image_tile]
    text_mid = own_f[:, image_tile:] + per_request(text_mod[:, 2], own_f, 0) * attn[:, image_tile:]
    image_local = modulate(image_mid, image_mod[:, 3], image_mod[:, 4], 0).astype(jnp.bfloat16)
    text_local = modulate(text_mid, text_mod[:, 3], text_mod[:, 4], 0).astype(jnp.bfloat16)
    ff_in = gather_slots(jnp.concatenate([image_local, text_local], 1), "head")
    image_hid = jax.nn.gelu(
        jnp.einsum("arnd,df->arnf", ff_in[:, :, :image_tile], image_up, preferred_element_type=jnp.float32),
        approximate=True,
    ).astype(jnp.bfloat16)
    text_hid = jax.nn.gelu(
        jnp.einsum("arnd,df->arnf", ff_in[:, :, image_tile:], text_up, preferred_element_type=jnp.float32),
        approximate=True,
    ).astype(jnp.bfloat16)
    image_back = jnp.einsum("arnf,fd->arnd", image_hid, image_down, preferred_element_type=jnp.float32)
    text_back = jnp.einsum("arnf,fd->arnd", text_hid, text_down, preferred_element_type=jnp.float32)
    mlp = scatter_slots(jnp.concatenate([image_back, text_back], 2).astype(jnp.bfloat16), "head")
    image_out = image_mid + per_request(image_mod[:, 5], image_mid, 0) * mlp[:, :image_tile]
    text_out = text_mid + per_request(text_mod[:, 5], text_mid, 0) * mlp[:, image_tile:]
    image_states = image_out.reshape(requests, tile_rows, tile_cols, model_width).astype(jnp.bfloat16)
    text_states = text_out.astype(jnp.bfloat16)
    final_in = modulate(image_out, final_mod[:, 1], final_mod[:, 0], 0).astype(jnp.bfloat16)
    velocity = jnp.einsum("rnd,dp->rnp", final_in, final_proj, preferred_element_type=jnp.float32)
    channels = velocity.shape[-1] // 4
    velocity = (
        velocity.reshape(requests, tile_rows, tile_cols, 2, 2, channels)
        .transpose(0, 1, 3, 2, 4, 5)
        .reshape(requests, 2 * tile_rows, 2 * tile_cols, channels)
    )
    current = step_index.astype(jnp.float32) / 1000.0
    following = jnp.maximum(step_index - 125, 0).astype(jnp.float32) / 1000.0
    step_size = noise_level(following) - noise_level(current)
    latent_next = latent_grid + step_size[:, None, None, None] * velocity
    decoded_in = (latent_next / 1.5305 + 0.0609).astype(jnp.bfloat16)
    padded = extended(decoded_in, (("head", 1), ("blk", 2)), 1)
    features = convolve(padded, conv_kernel)
    return (image_states, text_states, latent_next, features)


def solution(mesh):
    in_specs = (
        P("req", "head", "blk", None),
        P("req", ("head", "blk"), None),
        P("req", "head", "blk", None),
        P("req"),
        P("req"),
        P("req", None, None),
        P("req", None, None),
        P("req", None, None),
        P(),
        P(),
        P(None, None, "head"),
        P(None, None, "head"),
        P("head", None),
        P("head", None),
        P(None, "head"),
        P(None, "head"),
        P("head", None),
        P("head", None),
        P(),
        P(),
    )
    out_specs = (
        P("req", "head", "blk", None),
        P("req", ("head", "blk"), None),
        P("req", "head", "blk", None),
        P("req", "head", "blk", None),
    )
    return jax.shard_map(body, mesh=mesh, in_specs=in_specs, out_specs=out_specs, check_vma=False)
```
